32 devices in a mesh: dp: 4 (over x, core), label: 8 (over z, y).
Axes of the slice: x: 2, y: 2, z: 4, core: 2. Of those that a mesh axis runs over, the one named last changes fastest.
Arguments:
- token_ids: int32 [64, 2, 32], P(('dp', 'label')), may hold values from 0 to 4095
- labeled: int32 [64], P(('dp', 'label')), may hold values from 0 to 1, as said below
- positive_ids: int32 [64, 16], P(('dp', 'label')), may hold values from 0 to 163839
- vocab_table: bfloat16 [4096, 768], P(('dp', 'label')), may hold values from -6 to 6
- enc_weight: bfloat16 [768, 768], replicated, may hold values from -0.21875 to 0.21875
- label_matrix: bfloat16 [163840, 768], P(('dp', 'label')), may hold values from -0.21875 to 0.21875
- label_log_rates: float32 [163840], P(('dp', 'label')), may hold values from -11.5 to -6.9
Outputs:
- loss: float32 [], replicated
- grad_weight: float32 [768, 768], replicated
- new_log_rates: float32 [163840], P(('dp', 'label'))
The draws below stay inside these ranges and needn't reach their ends.
Inputs may be any that keep to these rules, and one draw needn't show every extreme that they name: At least one document has labeled = 1.
All inputs are finite; a program needn't handle non-finite values.
Results may differ from the reference program's by a relative error of at most 0.0042.
Values may be sent and summed in bfloat16 or wider, within the bound.
No kernel may reach another device: no remote copies, remote signals or barrier semaphores. Data moves between devices by JAX's collectives and lax.ppermute only.
A program may use at most 128 MiB of HBM per device.

```python
import math
import jax
import jax.numpy as jnp
import numpy as np
from jax import lax

D = 768
LAB_DEV = 5120
TITLE = 32
POS = 16
NL = 163840
VOCAB = 4096
DOCS = 64
N_DP = 4
N_LABEL = 8


def draw_labeled(key, part):
    flip_key, pick_key = jax.random.split(key)
    coin_flips = jax.random.randint(flip_key, (DOCS,), 0, 2, dtype=jnp.int32)
    chosen_doc = jax.random.randint(pick_key, (), 0, DOCS, dtype=jnp.int32)
    forced = (jnp.arange(DOCS, dtype=jnp.int32) == chosen_doc).astype(jnp.int32)
    return jnp.maximum(coin_flips, forced)


def plant(drawn, key, smallest, top_value):
    dims = drawn.shape
    index_at = [jax.random.randint(jax.random.fold_in(key, axis), (), 0, dims[axis]) for axis in range(len(dims))]
    drawn = drawn.at[tuple(index_at)].set(smallest)
    longest = dims.index(max(dims))
    index_at[longest] = (index_at[longest] + 1) % dims[longest]
    return drawn.at[tuple(index_at)].set(top_value)


def level_of(stream_key, dims, pieces, low, high):
    loudness = 1.0
    for axis_at, shards_of in pieces:
        heights = jax.random.uniform(jax.random.fold_in(jax.random.fold_in(stream_key, 6), axis_at), (shards_of,), jnp.float32, low / len(pieces), high / len(pieces))
        loudness = loudness * jnp.repeat(jnp.exp(heights), dims[axis_at] // shards_of).reshape((-1,) + (1,) * (len(dims) - 1 - axis_at))
    return loudness


def rank_bounds(count, skew):
    weights = [(1 << 20) // math.isqrt(rank ** skew) + 1 for rank in range(1, count + 1)]
    scale = 1 + sum(weights) // (1 << 30)
    return np.cumsum(np.array([max(1, weight // scale) for weight in weights]))


def ranked_ids(own_key, dims, number_of, lean):
    table = rank_bounds(number_of, lean)
    pick = jax.random.randint(jax.random.fold_in(own_key, 1), dims, 0, int(table[number_of - 1]))
    grade = jnp.searchsorted(jnp.asarray(table, jnp.int32), pick, side="right")
    return jax.random.permutation(jax.random.fold_in(own_key, 2), number_of)[grade].astype(jnp.int32)


def scatter_about(key, dims, spread, limit, pieces=(), kind=jnp.bfloat16):
    values = jax.random.normal(key, dims, jnp.float32) * spread
    if len(pieces) > 0:
        values = level_of(key, dims, pieces, -0.22, 0.18) * values
    return jnp.clip(values, min=-limit, max=limit).astype(kind)


def setup_inputs(seed: int = 0) -> dict:
    keys = jax.random.split(jax.random.key(seed), 8)
    token_ids = plant(ranked_ids(keys[0], (DOCS, 2, TITLE), VOCAB, 2), jax.random.fold_in(keys[0], 3), 0, VOCAB - 1).astype(jnp.int32)
    labeled = draw_labeled(jax.random.fold_in(keys[7], 71), 0)
    positive_ids = plant(jax.random.randint(keys[2], (DOCS, POS), 0, NL), jax.random.fold_in(keys[2], 1), 0, NL - 1).astype(jnp.int32)
    vocab_table = scatter_about(keys[3], (VOCAB, D), 1.0, 6.0, ((0, 32),))
    enc_weight = scatter_about(keys[4], (D, D), D ** -0.5, 0.21875)
    label_matrix = scatter_about(keys[5], (NL, D), D ** -0.5, 0.21875, ((0, 32),))
    label_log_rates = jnp.clip(-11.5 + 4.6 * jax.random.uniform(keys[6], (NL,), jnp.float32) ** level_of(keys[6], (NL,), ((0, 32),), -0.2, 0.2), -11.5, -6.9)
    return dict(token_ids=token_ids, labeled=labeled, positive_ids=positive_ids, vocab_table=vocab_table, enc_weight=enc_weight, label_matrix=label_matrix, label_log_rates=label_log_rates)


def reference(token_ids, labeled, positive_ids, vocab_table, enc_weight, label_matrix, label_log_rates):
    looked = vocab_table[token_ids].astype(jnp.float32)
    pooled = (lax.optimization_barrier(jnp.sum(looked, axis=2)) * (1.0 / TITLE)).astype(jnp.bfloat16)
    pooled = jnp.transpose(pooled, (1, 0, 2))
    flat = pooled.reshape(2 * DOCS, D)
    pre = jnp.dot(flat, enc_weight, preferred_element_type=jnp.float32)
    inv_norm = lax.rsqrt(lax.optimization_barrier(jnp.sum(pre * pre, axis=-1, keepdims=True)) + 1e-06)
    unit = pre * inv_norm
    emb = unit.astype(jnp.bfloat16)
    blocks = N_DP * N_LABEL
    label_blocks = label_matrix.reshape(blocks, LAB_DEV, D)
    rate_blocks = label_log_rates.reshape(blocks, LAB_DEV)
    starts = jnp.arange(blocks, dtype=jnp.int32) * LAB_DEV
    flag = (labeled == 1)[:, None]
    labeled_count = jnp.sum(labeled).astype(jnp.float32)

    def step(carry, inputs):
        total, loss_sum, grad_raw = carry
        block, log_rates, start = inputs
        scores = jnp.dot(emb, block.T, preferred_element_type=jnp.float32) * 16.0 - 6.0
        scores = scores.reshape(2, DOCS, LAB_DEV)
        weak = scores[0]
        strong = scores[1]
        teacher = jax.nn.sigmoid(weak)
        mean_teacher = lax.optimization_barrier(jnp.mean(teacher, axis=0))
        codes = start + jnp.arange(LAB_DEV, dtype=jnp.int32)
        hit = jnp.zeros((DOCS, LAB_DEV), dtype=bool)
        for column in range(POS):
            hit = hit | (positive_ids[:, column:column + 1] == codes[None, :])
        rates = jnp.exp(log_rates)
        target = jnp.where(flag, hit.astype(jnp.float32), teacher * rates[None, :] / mean_teacher[None, :])
        total = total + jnp.sum(target)
        loss_sum = loss_sum + jnp.sum(jax.nn.softplus(strong) - target * strong)
        slope = (jax.nn.sigmoid(strong) - target).astype(jnp.bfloat16)
        grad_raw = grad_raw + jnp.dot(slope, block, preferred_element_type=jnp.float32)
        batch_rate = lax.optimization_barrier(jnp.sum((flag & hit).astype(jnp.float32), axis=0)) / labeled_count
        new_block = jnp.log(0.9 * rates + 0.1 * batch_rate)
        return ((total, loss_sum, grad_raw), new_block)
    init = (jnp.zeros((), jnp.float32), jnp.zeros((), jnp.float32), jnp.zeros((DOCS, D), jnp.float32))
    (total, loss_sum, grad_raw), new_blocks = lax.scan(step, init, (label_blocks, rate_blocks, starts))
    grad_emb = grad_raw * (16.0 / total)
    unit_strong = unit[DOCS:]
    inv_strong = inv_norm[DOCS:]
    grad_pre = (grad_emb - unit_strong * lax.optimization_barrier(jnp.sum(unit_strong * grad_emb, axis=-1, keepdims=True))) * inv_strong
    pooled_strong = pooled[1].astype(jnp.float32)
    grad_weight = jnp.dot(pooled_strong.T, grad_pre, precision=lax.Precision.HIGHEST)
    loss = loss_sum / total
    return (loss, grad_weight, new_blocks.reshape(NL))
```

```python
import jax
import jax.numpy as jnp
from jax import lax
from jax.sharding import PartitionSpec as P

AXES = ("dp", "label")


def butterfly_sum(x, n):
    step = 1
    while step < n:
        x = x + lax.ppermute(x, AXES, [(i, i ^ step) for i in range(n)])
        step *= 2
    return x


def make_shards(n):
    def shards(
        token_ids, labeled, positive_ids, vocab_table, enc_weight, label_matrix, label_log_rates
    ):
        own_docs, views, title = token_ids.shape
        n_pos = positive_ids.shape[1]
        vocab_rows, width = vocab_table.shape
        label_rows = label_matrix.shape[0]
        me = lax.axis_index(AXES)
        docs = own_docs * n

        packed = jnp.concatenate(
            [token_ids.reshape(own_docs, views * title), positive_ids, labeled[:, None]], axis=1
        )
        slots = jnp.zeros((n, own_docs, packed.shape[1]), jnp.int32)
        slots = lax.dynamic_update_slice(slots, packed[None], (me, 0, 0))
        every = butterfly_sum(slots, n).reshape(docs, packed.shape[1])
        all_tokens = every[:, : views * title].reshape(docs, views, title)
        all_positives = every[:, views * title : views * title + n_pos]
        all_labeled = every[:, views * title + n_pos]

        rows = jnp.transpose(all_tokens, (1, 0, 2)).reshape(views * docs, title) - me * vocab_rows
        codes = jnp.arange(vocab_rows, dtype=jnp.int32)
        tally = jnp.zeros((views * docs, vocab_rows), jnp.float32)
        for position in range(title):
            tally = tally + (rows[:, position : position + 1] == codes[None, :]).astype(jnp.float32)
        partial = jnp.dot(tally.astype(jnp.bfloat16), vocab_table, preferred_element_type=jnp.float32)
        pooled = (butterfly_sum(partial, n) * (1.0 / title)).astype(jnp.bfloat16)

        pre = jnp.dot(pooled, enc_weight, preferred_element_type=jnp.float32)
        inv_norm = lax.rsqrt(jnp.sum(pre * pre, axis=-1, keepdims=True) + 1e-06)
        unit = pre * inv_norm
        emb = unit.astype(jnp.bfloat16)

        scores = (
            jnp.einsum("rk,lk->rl", emb, label_matrix, preferred_element_type=jnp.float32) * 16.0
            - 6.0
        )
        weak = scores[:docs]
        strong = scores[docs:]
        teacher = jax.nn.sigmoid(weak)
        mean_teacher = jnp.mean(teacher, axis=0)
        label_codes = me * label_rows + jnp.arange(label_rows, dtype=jnp.int32)
        hit = jnp.zeros((docs, label_rows), dtype=bool)
        for column in range(n_pos):
            hit = hit | (all_positives[:, column : column + 1] == label_codes[None, :])
        flag = (all_labeled == 1)[:, None]
        rates = jnp.exp(label_log_rates)
        target = jnp.where(
            flag, hit.astype(jnp.float32), teacher * rates[None, :] / mean_teacher[None, :]
        )
        total_local = jnp.sum(target)
        loss_local = jnp.sum(jax.nn.softplus(strong) - target * strong)
        slope = (jax.nn.sigmoid(strong) - target).astype(jnp.bfloat16)
        labeled_count = jnp.sum(all_labeled).astype(jnp.float32)
        batch_rate = jnp.sum((flag & hit).astype(jnp.float32), axis=0) / labeled_count
        new_log_rates = jnp.log(0.9 * rates + 0.1 * batch_rate)

        grad_local = jnp.dot(slope, label_matrix, preferred_element_type=jnp.float32)
        extra = jnp.zeros((1, width), jnp.float32).at[0, 0].set(total_local).at[0, 1].set(loss_local)
        summed = butterfly_sum(jnp.concatenate([grad_local, extra], axis=0), n)
        total = summed[docs, 0]
        loss_sum = summed[docs, 1]
        grad_emb = summed[:docs] * (16.0 / total)
        unit_strong = unit[docs:]
        grad_pre = (
            grad_emb - unit_strong * jnp.sum(unit_strong * grad_emb, axis=-1, keepdims=True)
        ) * inv_norm[docs:]
        grad_weight = jnp.einsum(
            "dk,dj->kj", pooled[docs:].astype(jnp.float32), grad_pre, precision=lax.Precision.HIGHEST
        )
        loss = loss_sum / total
        return (loss, grad_weight, new_log_rates)

    return shards


def solution(mesh):
    n = mesh.shape["dp"] * mesh.shape["label"]
    assert n & (n - 1) == 0, "n not pow2"
    return jax.shard_map(
        make_shards(n),
        mesh=mesh,
        in_specs=(
            P(AXES, None, None),
            P(AXES),
            P(AXES, None),
            P(AXES, None),
            P(),
            P(AXES, None),
            P(AXES),
        ),
        out_specs=(P(), P(), P(AXES)),
        check_vma=False,
    )
```

```python
import jax
import jax.numpy as jnp
from jax import lax
from jax.sharding import PartitionSpec as P

AXES = ("dp", "label")


def butterfly_sum(x, n, pair_step=0):
    if pair_step:
        me = lax.axis_index(AXES)
        upper = (me // pair_step) % 2 == 1
        half = x.shape[1] // 2
        low, high = x[:, :half], x[:, half:]
        swap = [(i, i ^ pair_step) for i in range(n)]
        x = jnp.where(upper, high, low) + lax.ppermute(jnp.where(upper, low, high), AXES, swap)
    step = 1
    while step < n:
        if step != pair_step:
            x = x + lax.ppermute(x, AXES, [(i, i ^ step) for i in range(n)])
        step *= 2
    if pair_step:
        other = lax.ppermute(x, AXES, swap)
        x = jnp.where(upper, jnp.concatenate([other, x], 1), jnp.concatenate([x, other], 1))
    return x


def make_shards(n, pair_step):
    def shards(
        token_ids, labeled, positive_ids, vocab_table, enc_weight, label_matrix, label_log_rates
    ):
        own_docs, views, title = token_ids.shape
        n_pos = positive_ids.shape[1]
        vocab_rows, width = vocab_table.shape
        label_rows = label_matrix.shape[0]
        me = lax.axis_index(AXES)
        docs = own_docs * n

        packed = jnp.concatenate(
            [token_ids.reshape(own_docs, views * title), positive_ids, labeled[:, None]], axis=1
        )
        slots = jnp.zeros((n, own_docs, packed.shape[1]), jnp.int32)
        slots = lax.dynamic_update_slice(slots, packed[None], (me, 0, 0))
        every = butterfly_sum(slots, n).reshape(docs, packed.shape[1])
        all_tokens = every[:, : views * title].reshape(docs, views, title)
        all_positives = every[:, views * title : views * title + n_pos]
        all_labeled = every[:, views * title + n_pos]

        rows = jnp.transpose(all_tokens, (1, 0, 2)).reshape(views * docs, title) - me * vocab_rows
        codes = jnp.arange(vocab_rows, dtype=jnp.int32)
        tally = jnp.zeros((views * docs, vocab_rows), jnp.float32)
        for position in range(title):
            tally = tally + (rows[:, position : position + 1] == codes[None, :]).astype(jnp.float32)
        partial = jnp.dot(tally.astype(jnp.bfloat16), vocab_table, preferred_element_type=jnp.float32)
        pooled = (butterfly_sum(partial, n, pair_step) * (1.0 / title)).astype(jnp.bfloat16)

        pre = jnp.dot(pooled, enc_weight, preferred_element_type=jnp.float32)
        inv_norm = lax.rsqrt(jnp.sum(pre * pre, axis=-1, keepdims=True) + 1e-06)
        unit = pre * inv_norm
        emb = unit.astype(jnp.bfloat16)

        scores = (
            jnp.einsum("rk,lk->rl", emb, label_matrix, preferred_element_type=jnp.float32) * 16.0
            - 6.0
        )
        weak = scores[:docs]
        strong = scores[docs:]
        teacher = jax.nn.sigmoid(weak)
        mean_teacher = jnp.mean(teacher, axis=0)
        label_codes = me * label_rows + jnp.arange(label_rows, dtype=jnp.int32)
        hit = jnp.zeros((docs, label_rows), dtype=bool)
        for column in range(n_pos):
            hit = hit | (all_positives[:, column : column + 1] == label_codes[None, :])
        flag = (all_labeled == 1)[:, None]
        rates = jnp.exp(label_log_rates)
        target = jnp.where(
            flag, hit.astype(jnp.float32), teacher * rates[None, :] / mean_teacher[None, :]
        )
        total_local = jnp.sum(target)
        loss_local = jnp.sum(jax.nn.softplus(strong) - target * strong)
        slope = (jax.nn.sigmoid(strong) - target).astype(jnp.bfloat16)
        labeled_count = jnp.sum(all_labeled).astype(jnp.float32)
        batch_rate = jnp.sum((flag & hit).astype(jnp.float32), axis=0) / labeled_count
        new_log_rates = jnp.log(0.9 * rates + 0.1 * batch_rate)

        grad_local = jnp.dot(slope, label_matrix, preferred_element_type=jnp.float32)
        lane = jnp.arange(width, dtype=jnp.int32)[None, :]
        extra = jnp.where(lane == 0, total_local, jnp.where(lane == 1, loss_local, 0.0))
        summed = butterfly_sum(jnp.concatenate([grad_local, extra], axis=0), n, pair_step)
        total = summed[docs, 0]
        loss_sum = summed[docs, 1]
        grad_emb = summed[:docs] * (16.0 / total)
        unit_strong = unit[docs:]
        grad_pre = (
            grad_emb - unit_strong * jnp.sum(unit_strong * grad_emb, axis=-1, keepdims=True)
        ) * inv_norm[docs:]
        grad_weight = jnp.einsum(
            "dk,dj->kj", pooled[docs:].astype(jnp.float32), grad_pre, precision=lax.Precision.HIGHEST
        )
        loss = loss_sum / total
        return (loss, grad_weight, new_log_rates)

    return shards


def solution(mesh):
    n = mesh.shape["dp"] * mesh.shape["label"]
    assert n & (n - 1) == 0, "n not pow2"
    return jax.shard_map(
        make_shards(n, mesh.shape["label"]),
        mesh=mesh,
        in_specs=(
            P(AXES, None, None),
            P(AXES),
            P(AXES, None),
            P(AXES, None),
            P(),
            P(AXES, None),
            P(AXES),
        ),
        out_specs=(P(), P(), P(AXES)),
        check_vma=False,
    )
```

```python
import jax
import jax.numpy as jnp
from jax import lax
from jax.sharding import PartitionSpec as P

AXES = ("dp", "label")


def tree_sum(x, n, n_label):
    me = lax.axis_index(AXES)
    upper = (me // n_label) % 2 == 1
    half = x.shape[1] // 2
    low, high = x[:, :half], x[:, half:]
    swap = [(i, i ^ n_label) for i in range(n)]
    x = jnp.where(upper, high, low) + lax.ppermute(jnp.where(upper, low, high), AXES, swap)
    rows = x.shape[0]
    part = lax.all_to_all(x.reshape(n_label, rows // n_label, half), "label", 0, 0, tiled=False)
    part = jnp.sum(part, axis=0)
    step = 2 * n_label
    while step < n:
        part = part + lax.ppermute(part, AXES, [(i, i ^ step) for i in range(n)])
        step *= 2
    every = jnp.broadcast_to(part[None], (n_label,) + part.shape)
    x = lax.all_to_all(every, "label", 0, 0, tiled=False).reshape(rows, half)
    other = lax.ppermute(x, AXES, swap)
    return jnp.where(upper, jnp.concatenate([other, x], 1), jnp.concatenate([x, other], 1))


def make_shards(n, n_label):
    def shards(
        token_ids, labeled, positive_ids, vocab_table, enc_weight, label_matrix, label_log_rates
    ):
        own_docs, views, title = token_ids.shape
        n_pos = positive_ids.shape[1]
        vocab_rows, width = vocab_table.shape
        label_rows = label_matrix.shape[0]
        me = lax.axis_index(AXES)
        docs = own_docs * n

        packed = jnp.concatenate(
            [token_ids.reshape(own_docs, views * title), positive_ids, labeled[:, None]], axis=1
        )
        spread = jnp.broadcast_to(packed[None], (n,) + packed.shape)
        every = lax.all_to_all(spread, AXES, 0, 0, tiled=False).reshape(docs, packed.shape[1])
        all_tokens = every[:, : views * title].reshape(docs, views, title)
        all_positives = every[:, views * title : views * title + n_pos]
        all_labeled = every[:, views * title + n_pos]

        rows = jnp.transpose(all_tokens, (1, 0, 2)).reshape(views * docs, title) - me * vocab_rows
        codes = jnp.arange(vocab_rows, dtype=jnp.int32)
        tally = jnp.zeros((views * docs, vocab_rows), jnp.float32)
        for position in range(title):
            tally = tally + (rows[:, position : position + 1] == codes[None, :]).astype(jnp.float32)
        partial = jnp.dot(tally.astype(jnp.bfloat16), vocab_table, preferred_element_type=jnp.float32)
        pooled = (tree_sum(partial, n, n_label) * (1.0 / title)).astype(jnp.bfloat16)

        pre = jnp.dot(pooled, enc_weight, preferred_element_type=jnp.float32)
        inv_norm = lax.rsqrt(jnp.sum(pre * pre, axis=-1, keepdims=True) + 1e-06)
        unit = pre * inv_norm
        emb = unit.astype(jnp.bfloat16)

        scores = (
            jnp.einsum("rk,lk->rl", emb, label_matrix, preferred_element_type=jnp.float32) * 16.0
            - 6.0
        )
        weak = scores[:docs]
        strong = scores[docs:]
        teacher = jax.nn.sigmoid(weak)
        mean_teacher = jnp.mean(teacher, axis=0)
        label_codes = me * label_rows + jnp.arange(label_rows, dtype=jnp.int32)
        hit = jnp.zeros((docs, label_rows), dtype=bool)
        for column in range(n_pos):
            hit = hit | (all_positives[:, column : column + 1] == label_codes[None, :])
        flag = (all_labeled == 1)[:, None]
        rates = jnp.exp(label_log_rates)
        target = jnp.where(
            flag, hit.astype(jnp.float32), teacher * rates[None, :] / mean_teacher[None, :]
        )
        total_local = jnp.sum(target)
        loss_local = jnp.sum(jax.nn.softplus(strong) - target * strong)
        slope = (jax.nn.sigmoid(strong) - target).astype(jnp.bfloat16)
        labeled_count = jnp.sum(all_labeled).astype(jnp.float32)
        batch_rate = jnp.sum((flag & hit).astype(jnp.float32), axis=0) / labeled_count
        new_log_rates = jnp.log(0.9 * rates + 0.1 * batch_rate)

        grad_local = jnp.dot(slope, label_matrix, preferred_element_type=jnp.float32)
        lane = jnp.arange(width, dtype=jnp.int32)[None, :]
        extra = jnp.where(lane == 0, total_local, jnp.where(lane == 1, loss_local, 0.0))
        pad = jnp.zeros((n_label - 1 - (docs % n_label), width), jnp.float32)
        summed = tree_sum(jnp.concatenate([grad_local, extra, pad], axis=0), n, n_label)
        total = summed[docs, 0]
        loss_sum = summed[docs, 1]
        grad_emb = summed[:docs] * (16.0 / total)
        unit_strong = unit[docs:]
        grad_pre = (
            grad_emb - unit_strong * jnp.sum(unit_strong * grad_emb, axis=-1, keepdims=True)
        ) * inv_norm[docs:]
        grad_weight = jnp.einsum(
            "dk,dj->kj", pooled[docs:].astype(jnp.float32), grad_pre, precision=lax.Precision.HIGHEST
        )
        loss = loss_sum / total
        return (loss, grad_weight, new_log_rates)

    return shards


def solution(mesh):
    n = mesh.shape["dp"] * mesh.shape["label"]
    assert n & (n - 1) == 0, "n not pow2"
    return jax.shard_map(
        make_shards(n, mesh.shape["label"]),
        mesh=mesh,
        in_specs=(
            P(AXES, None, None),
            P(AXES),
            P(AXES, None),
            P(AXES, None),
            P(),
            P(AXES, None),
            P(AXES),
        ),
        out_specs=(P(), P(), P(AXES)),
        check_vma=False,
    )
```

```python
import jax
import jax.numpy as jnp
from jax import lax
from jax.sharding import PartitionSpec as P

AXES = ("dp", "label")


def tree_sum(x, n, n_label):
    me = lax.axis_index(AXES)
    upper = (me // n_label) % 2 == 1
    half = x.shape[1] // 2
    low, high = x[:, :half], x[:, half:]
    swap = [(i, i ^ n_label) for i in range(n)]
    x = jnp.where(upper, high, low) + lax.ppermute(jnp.where(upper, low, high), AXES, swap)
    rows = x.shape[0]
    part = lax.all_to_all(x.reshape(n_label, rows // n_label, half), "label", 0, 0, tiled=False)
    part = jnp.sum(part, axis=0)
    step = 2 * n_label
    while step < n:
        part = part + lax.ppermute(part, AXES, [(i, i ^ step) for i in range(n)])
        step *= 2
    every = jnp.broadcast_to(part[None], (n_label,) + part.shape)
    x = lax.all_to_all(every, "label", 0, 0, tiled=False).reshape(rows, half)
    other = lax.ppermute(x, AXES, swap)
    return jnp.where(upper, jnp.concatenate([other, x], 1), jnp.concatenate([x, other], 1))


def butterfly_sum(x, n, pair_step):
    me = lax.axis_index(AXES)
    upper = (me // pair_step) % 2 == 1
    half = x.shape[1] // 2
    low, high = x[:, :half], x[:, half:]
    swap = [(i, i ^ pair_step) for i in range(n)]
    x = jnp.where(upper, high, low) + lax.ppermute(jnp.where(upper, low, high), AXES, swap)
    step = 1
    while step < n:
        if step != pair_step:
            x = x + lax.ppermute(x, AXES, [(i, i ^ step) for i in range(n)])
        step *= 2
    other = lax.ppermute(x, AXES, swap)
    return jnp.where(upper, jnp.concatenate([other, x], 1), jnp.concatenate([x, other], 1))


def make_shards(n, n_label):
    def shards(
        token_ids, labeled, positive_ids, vocab_table, enc_weight, label_matrix, label_log_rates
    ):
        own_docs, views, title = token_ids.shape
        n_pos = positive_ids.shape[1]
        vocab_rows, width = vocab_table.shape
        label_rows = label_matrix.shape[0]
        me = lax.axis_index(AXES)
        docs = own_docs * n

        packed = jnp.concatenate(
            [token_ids.reshape(own_docs, views * title), positive_ids, labeled[:, None]], axis=1
        )
        spread = jnp.broadcast_to(packed[None], (n,) + packed.shape)
        every = lax.all_to_all(spread, AXES, 0, 0, tiled=False).reshape(docs, packed.shape[1])
        all_tokens = every[:, : views * title].reshape(docs, views, title)
        all_positives = every[:, views * title : views * title + n_pos]
        all_labeled = every[:, views * title + n_pos]

        rows = jnp.transpose(all_tokens, (1, 0, 2)).reshape(views * docs, title) - me * vocab_rows
        codes = jnp.arange(vocab_rows, dtype=jnp.int32)
        tally = jnp.zeros((views * docs, vocab_rows), jnp.float32)
        for position in range(title):
            tally = tally + (rows[:, position : position + 1] == codes[None, :]).astype(jnp.float32)
        partial = jnp.dot(tally.astype(jnp.bfloat16), vocab_table, preferred_element_type=jnp.float32)
        pooled = (tree_sum(partial, n, n_label) * (1.0 / title)).astype(jnp.bfloat16)

        pre = jnp.dot(pooled, enc_weight, preferred_element_type=jnp.float32)
        inv_norm = lax.rsqrt(jnp.sum(pre * pre, axis=-1, keepdims=True) + 1e-06)
        unit = pre * inv_norm
        emb = unit.astype(jnp.bfloat16)

        scores = (
            jnp.einsum("rk,lk->rl", emb, label_matrix, preferred_element_type=jnp.float32) * 16.0
            - 6.0
        )
        weak = scores[:docs]
        strong = scores[docs:]
        teacher = jax.nn.sigmoid(weak)
        mean_teacher = jnp.mean(teacher, axis=0)
        label_codes = me * label_rows + jnp.arange(label_rows, dtype=jnp.int32)
        hit = jnp.zeros((docs, label_rows), dtype=bool)
        for column in range(n_pos):
            hit = hit | (all_positives[:, column : column + 1] == label_codes[None, :])
        flag = (all_labeled == 1)[:, None]
        rates = jnp.exp(label_log_rates)
        target = jnp.where(
            flag, hit.astype(jnp.float32), teacher * rates[None, :] / mean_teacher[None, :]
        )
        total_local = jnp.sum(target)
        loss_local = jnp.sum(jax.nn.softplus(strong) - target * strong)
        slope = (jax.nn.sigmoid(strong) - target).astype(jnp.bfloat16)
        labeled_count = jnp.sum(all_labeled).astype(jnp.float32)
        batch_rate = jnp.sum((flag & hit).astype(jnp.float32), axis=0) / labeled_count
        new_log_rates = jnp.log(0.9 * rates + 0.1 * batch_rate)

        grad_local = jnp.dot(slope, label_matrix, preferred_element_type=jnp.float32)
        lane = jnp.arange(width, dtype=jnp.int32)[None, :]
        extra = jnp.where(lane == 0, total_local, jnp.where(lane == 1, loss_local, 0.0))
        summed = butterfly_sum(jnp.concatenate([grad_local, extra], axis=0), n, n_label)
        total = summed[docs, 0]
        loss_sum = summed[docs, 1]
        grad_emb = summed[:docs] * (16.0 / total)
        unit_strong = unit[docs:]
        grad_pre = (
            grad_emb - unit_strong * jnp.sum(unit_strong * grad_emb, axis=-1, keepdims=True)
        ) * inv_norm[docs:]
        grad_weight = jnp.einsum(
            "dk,dj->kj", pooled[docs:].astype(jnp.float32), grad_pre, precision=lax.Precision.HIGHEST
        )
        loss = loss_sum / total
        return (loss, grad_weight, new_log_rates)

    return shards


def solution(mesh):
    n = mesh.shape["dp"] * mesh.shape["label"]
    assert n & (n - 1) == 0, "n not pow2"
    return jax.shard_map(
        make_shards(n, mesh.shape["label"]),
        mesh=mesh,
        in_specs=(
            P(AXES, None, None),
            P(AXES),
            P(AXES, None),
            P(AXES, None),
            P(),
            P(AXES, None),
            P(AXES),
        ),
        out_specs=(P(), P(), P(AXES)),
        check_vma=False,
    )
```

```python
import jax
import jax.numpy as jnp
from jax import lax
from jax.experimental import pallas as pl
from jax.experimental.pallas import tpu as pltpu
from jax.sharding import PartitionSpec as P

AXES = ("dp", "label")


def tree_sum(x, n, n_label):
    me = lax.axis_index(AXES)
    upper = (me // n_label) % 2 == 1
    half = x.shape[1] // 2
    low, high = x[:, :half], x[:, half:]
    swap = [(i, i ^ n_label) for i in range(n)]
    x = jnp.where(upper, high, low) + lax.ppermute(jnp.where(upper, low, high), AXES, swap)
    rows = x.shape[0]
    part = lax.all_to_all(x.reshape(n_label, rows // n_label, half), "label", 0, 0, tiled=False)
    part = jnp.sum(part, axis=0)
    step = 2 * n_label
    while step < n:
        part = part + lax.ppermute(part, AXES, [(i, i ^ step) for i in range(n)])
        step *= 2
    every = jnp.broadcast_to(part[None], (n_label,) + part.shape)
    x = lax.all_to_all(every, "label", 0, 0, tiled=False).reshape(rows, half)
    other = lax.ppermute(x, AXES, swap)
    return jnp.where(upper, jnp.concatenate([other, x], 1), jnp.concatenate([x, other], 1))


def butterfly_sum(x, n, pair_step):
    me = lax.axis_index(AXES)
    upper = (me // pair_step) % 2 == 1
    half = x.shape[1] // 2
    low, high = x[:, :half], x[:, half:]
    swap = [(i, i ^ pair_step) for i in range(n)]
    x = jnp.where(upper, high, low) + lax.ppermute(jnp.where(upper, low, high), AXES, swap)
    step = 1
    while step < n:
        if step != pair_step:
            x = x + lax.ppermute(x, AXES, [(i, i ^ step) for i in range(n)])
        step *= 2
    other = lax.ppermute(x, AXES, swap)
    return jnp.where(upper, jnp.concatenate([other, x], 1), jnp.concatenate([x, other], 1))


def label_kernel(emb_ref, lab_ref, rate_ref, pos_ref, flag_ref, grad_ref, cols_ref):
    tile = pl.program_id(0)
    docs = pos_ref.shape[0]
    width = lab_ref.shape[0]
    lab = lab_ref[...]
    scores = (
        lax.dot_general(emb_ref[...], lab, (((1,), (1,)), ((), ())), preferred_element_type=jnp.float32)
        * 16.0
        - 6.0
    )
    weak = scores[:docs]
    strong = scores[docs:]
    teacher = jax.nn.sigmoid(weak)
    mean_teacher = jnp.sum(teacher, axis=0, keepdims=True) / docs
    codes = tile * width + lax.broadcasted_iota(jnp.int32, (1, width), 1)
    pos = pos_ref[...]
    hit = pos[:, 0:1] == codes
    for column in range(1, pos.shape[1]):
        hit = hit | (pos[:, column : column + 1] == codes)
    hit = hit.astype(jnp.float32)
    flag = flag_ref[...]
    target = jnp.where(flag > 0.5, hit, teacher * rate_ref[...] / mean_teacher)
    softplus = jnp.maximum(strong, 0.0) + jnp.log1p(jnp.exp(-jnp.abs(strong)))
    slope = (jax.nn.sigmoid(strong) - target).astype(jnp.bfloat16)
    cols_ref[0:1, :] = jnp.sum(target, axis=0, keepdims=True)
    cols_ref[1:2, :] = jnp.sum(softplus - target * strong, axis=0, keepdims=True)
    cols_ref[2:3, :] = jnp.sum(flag * hit, axis=0, keepdims=True)
    part = jnp.dot(slope, lab, preferred_element_type=jnp.float32)

    @pl.when(tile == 0)
    def _():
        grad_ref[...] = part

    @pl.when(tile > 0)
    def _():
        grad_ref[...] += part


def label_pass(emb, label_matrix, rates, positives, flag):
    rows, depth = emb.shape
    docs, n_pos = positives.shape
    labels = label_matrix.shape[0]
    width = 1024 if labels % 1024 == 0 else labels
    return pl.pallas_call(
        label_kernel,
        grid=(labels // width,),
        in_specs=[
            pl.BlockSpec((rows, depth), lambda i: (0, 0)),
            pl.BlockSpec((width, depth), lambda i: (i, 0)),
            pl.BlockSpec((1, width), lambda i: (0, i)),
            pl.BlockSpec((docs, n_pos), lambda i: (0, 0)),
            pl.BlockSpec((docs, 1), lambda i: (0, 0)),
        ],
        out_specs=[
            pl.BlockSpec((docs, depth), lambda i: (0, 0)),
            pl.BlockSpec((3, width), lambda i: (0, i)),
        ],
        out_shape=[
            jax.ShapeDtypeStruct((docs, depth), jnp.float32),
            jax.ShapeDtypeStruct((3, labels), jnp.float32),
        ],
        compiler_params=pltpu.CompilerParams(dimension_semantics=("arbitrary",)),
    )(emb, label_matrix, rates, positives, flag)


def make_shards(n, n_label):
    def shards(
        token_ids, labeled, positive_ids, vocab_table, enc_weight, label_matrix, label_log_rates
    ):
        own_docs, views, title = token_ids.shape
        n_pos = positive_ids.shape[1]
        vocab_rows, width = vocab_table.shape
        label_rows = label_matrix.shape[0]
        me = lax.axis_index(AXES)
        docs = own_docs * n

        packed = jnp.concatenate(
            [token_ids.reshape(own_docs, views * title), positive_ids, labeled[:, None]], axis=1
        )
        spread = jnp.broadcast_to(packed[None], (n,) + packed.shape)
        every = lax.all_to_all(spread, AXES, 0, 0, tiled=False).reshape(docs, packed.shape[1])
        all_tokens = every[:, : views * title].reshape(docs, views, title)
        all_positives = every[:, views * title : views * title + n_pos]
        all_labeled = every[:, views * title + n_pos]

        rows = jnp.transpose(all_tokens, (1, 0, 2)).reshape(views * docs, title) - me * vocab_rows
        codes = jnp.arange(vocab_rows, dtype=jnp.int32)
        tally = jnp.zeros((views * docs, vocab_rows), jnp.float32)
        for position in range(title):
            tally = tally + (rows[:, position : position + 1] == codes[None, :]).astype(jnp.float32)
        partial = jnp.dot(tally.astype(jnp.bfloat16), vocab_table, preferred_element_type=jnp.float32)
        pooled = (tree_sum(partial, n, n_label) * (1.0 / title)).astype(jnp.bfloat16)

        pre = jnp.dot(pooled, enc_weight, preferred_element_type=jnp.float32)
        inv_norm = lax.rsqrt(jnp.sum(pre * pre, axis=-1, keepdims=True) + 1e-06)
        unit = pre * inv_norm
        emb = unit.astype(jnp.bfloat16)

        rates = jnp.exp(label_log_rates)
        flag = (all_labeled == 1).astype(jnp.float32)[:, None]
        grad_local, cols = label_pass(
            emb, label_matrix, rates[None, :], all_positives - me * label_rows, flag
        )
        total_local = jnp.sum(cols[0])
        loss_local = jnp.sum(cols[1])
        labeled_count = jnp.sum(all_labeled).astype(jnp.float32)
        batch_rate = cols[2] / labeled_count
        new_log_rates = jnp.log(0.9 * rates + 0.1 * batch_rate)

        lane = jnp.arange(width, dtype=jnp.int32)[None, :]
        extra = jnp.where(lane == 0, total_local, jnp.where(lane == 1, loss_local, 0.0))
        summed = butterfly_sum(jnp.concatenate([grad_local, extra], axis=0), n, n_label)
        total = summed[docs, 0]
        loss_sum = summed[docs, 1]
        grad_emb = summed[:docs] * (16.0 / total)
        unit_strong = unit[docs:]
        grad_pre = (
            grad_emb - unit_strong * jnp.sum(unit_strong * grad_emb, axis=-1, keepdims=True)
        ) * inv_norm[docs:]
        grad_weight = jnp.einsum(
            "dk,dj->kj", pooled[docs:].astype(jnp.float32), grad_pre, precision=lax.Precision.HIGHEST
        )
        loss = loss_sum / total
        return (loss, grad_weight, new_log_rates)

    return shards


def solution(mesh):
    n = mesh.shape["dp"] * mesh.shape["label"]
    assert n & (n - 1) == 0, "n not pow2"
    return jax.shard_map(
        make_shards(n, mesh.shape["label"]),
        mesh=mesh,
        in_specs=(
            P(AXES, None, None),
            P(AXES),
            P(AXES, None),
            P(AXES, None),
            P(),
            P(AXES, None),
            P(AXES),
        ),
        out_specs=(P(), P(), P(AXES)),
        check_vma=False,
    )
```

```python
import jax
import jax.numpy as jnp
from jax import lax
from jax.experimental import pallas as pl
from jax.experimental.pallas import tpu as pltpu
from jax.sharding import PartitionSpec as P

AXES = ("dp", "label")


def tree_sum(x, n, n_label):
    me = lax.axis_index(AXES)
    upper = (me // n_label) % 2 == 1
    half = x.shape[1] // 2
    low, high = x[:, :half], x[:, half:]
    swap = [(i, i ^ n_label) for i in range(n)]
    x = jnp.where(upper, high, low) + lax.ppermute(jnp.where(upper, low, high), AXES, swap)
    rows = x.shape[0]
    part = lax.all_to_all(x.reshape(n_label, rows // n_label, half), "label", 0, 0, tiled=False)
    part = jnp.sum(part, axis=0)
    step = 2 * n_label
    while step < n:
        part = part + lax.ppermute(part, AXES, [(i, i ^ step) for i in range(n)])
        step *= 2
    every = jnp.broadcast_to(part[None], (n_label,) + part.shape)
    x = lax.all_to_all(every, "label", 0, 0, tiled=False).reshape(rows, half)
    other = lax.ppermute(x, AXES, swap)
    return jnp.where(upper, jnp.concatenate([other, x], 1), jnp.concatenate([x, other], 1))


def label_kernel(place_ref, emb_ref, lab_ref, rate_ref, ints_ref, keep_ref, send_ref, rate_out_ref):
    tile = pl.program_id(0)
    upper = place_ref[0] == 1
    base = place_ref[1]
    docs, half = send_ref.shape[0] - 8, send_ref.shape[1]
    width = lab_ref.shape[0]
    n_pos = ints_ref.shape[1] - 1
    lab = lab_ref[...]
    scores = (
        lax.dot_general(emb_ref[...], lab, (((1,), (1,)), ((), ())), preferred_element_type=jnp.float32)
        * 16.0
        - 6.0
    )
    weak = scores[:docs]
    strong = scores[docs:]
    teacher = jax.nn.sigmoid(weak)
    mean_teacher = jnp.sum(teacher, axis=0, keepdims=True) / docs
    codes = base + tile * width + lax.broadcasted_iota(jnp.int32, (1, width), 1)
    ints = ints_ref[...]
    hit = ints[:, 0:1] == codes
    for column in range(1, n_pos):
        hit = hit | (ints[:, column : column + 1] == codes)
    hit = hit.astype(jnp.float32)
    flag = (ints[:, n_pos : n_pos + 1] == 1).astype(jnp.float32)
    target = jnp.where(flag > 0.5, hit, teacher * rate_ref[...] / mean_teacher)
    softplus = jnp.maximum(strong, 0.0) + jnp.log1p(jnp.exp(-jnp.abs(strong)))
    slope = (jax.nn.sigmoid(strong) - target).astype(jnp.bfloat16)
    rate_out_ref[...] = jnp.sum(flag * hit, axis=0, keepdims=True)
    part = jnp.dot(slope, lab, preferred_element_type=jnp.float32)
    low, high = part[:, :half], part[:, half:]
    lane = lax.broadcasted_iota(jnp.int32, (8, half), 1)
    row = lax.broadcasted_iota(jnp.int32, (8, half), 0)
    total = jnp.sum(target)
    loss = jnp.sum(softplus - target * strong)
    extra = jnp.where(row == 0, jnp.where(lane == 0, total, jnp.where(lane == 1, loss, 0.0)), 0.0)
    keep = jnp.concatenate([jnp.where(upper, high, low), jnp.where(upper, 0.0, extra)], axis=0)
    send = jnp.concatenate([jnp.where(upper, low, high), jnp.where(upper, extra, 0.0)], axis=0)

    @pl.when(tile == 0)
    def _():
        keep_ref[...] = keep
        send_ref[...] = send

    @pl.when(tile > 0)
    def _():
        keep_ref[...] += keep
        send_ref[...] += send


def label_pass(place, emb, label_matrix, rates, ints):
    rows, depth = emb.shape
    docs = ints.shape[0]
    labels = label_matrix.shape[0]
    width = 1024 if labels % 1024 == 0 else labels
    half = depth // 2
    return pl.pallas_call(
        label_kernel,
        grid_spec=pltpu.PrefetchScalarGridSpec(
            num_scalar_prefetch=1,
            grid=(labels // width,),
            in_specs=[
                pl.BlockSpec((rows, depth), lambda i, p: (0, 0)),
                pl.BlockSpec((width, depth), lambda i, p: (i, 0)),
                pl.BlockSpec((1, width), lambda i, p: (0, i)),
                pl.BlockSpec(ints.shape, lambda i, p: (0, 0)),
            ],
            out_specs=[
                pl.BlockSpec((docs + 8, half), lambda i, p: (0, 0)),
                pl.BlockSpec((docs + 8, half), lambda i, p: (0, 0)),
                pl.BlockSpec((1, width), lambda i, p: (0, i)),
            ],
        ),
        out_shape=[
            jax.ShapeDtypeStruct((docs + 8, half), jnp.float32),
            jax.ShapeDtypeStruct((docs + 8, half), jnp.float32),
            jax.ShapeDtypeStruct((1, labels), jnp.float32),
        ],
        compiler_params=pltpu.CompilerParams(dimension_semantics=("arbitrary",)),
    )(place, emb, label_matrix, rates, ints)


def split_sum(keep, send, n, pair_step):
    me = lax.axis_index(AXES)
    upper = (me // pair_step) % 2 == 1
    swap = [(i, i ^ pair_step) for i in range(n)]
    x = keep + lax.ppermute(send, AXES, swap)
    step = 1
    while step < n:
        if step != pair_step:
            x = x + lax.ppermute(x, AXES, [(i, i ^ step) for i in range(n)])
        step *= 2
    other = lax.ppermute(x, AXES, swap)
    return jnp.where(upper, jnp.concatenate([other, x], 1), jnp.concatenate([x, other], 1))


def make_shards(n, n_label):
    def shards(
        token_ids, labeled, positive_ids, vocab_table, enc_weight, label_matrix, label_log_rates
    ):
        own_docs, views, title = token_ids.shape
        n_pos = positive_ids.shape[1]
        vocab_rows, width = vocab_table.shape
        label_rows = label_matrix.shape[0]
        me = lax.axis_index(AXES)
        docs = own_docs * n

        packed = jnp.concatenate(
            [token_ids.reshape(own_docs, views * title), positive_ids, labeled[:, None]], axis=1
        )
        spread = jnp.broadcast_to(packed[None], (n,) + packed.shape)
        every = lax.all_to_all(spread, AXES, 0, 0, tiled=False).reshape(docs, packed.shape[1])
        all_tokens = every[:, : views * title].reshape(docs, views, title)
        all_labeled = every[:, views * title + n_pos]

        rows = jnp.transpose(all_tokens, (1, 0, 2)).reshape(views * docs, title) - me * vocab_rows
        codes = jnp.arange(vocab_rows, dtype=jnp.int32)
        tally = jnp.zeros((views * docs, vocab_rows), jnp.float32)
        for position in range(title):
            tally = tally + (rows[:, position : position + 1] == codes[None, :]).astype(jnp.float32)
        partial = jnp.dot(tally.astype(jnp.bfloat16), vocab_table, preferred_element_type=jnp.float32)
        pooled = (tree_sum(partial, n, n_label) * (1.0 / title)).astype(jnp.bfloat16)

        pre = jnp.dot(pooled, enc_weight, preferred_element_type=jnp.float32)
        inv_norm = lax.rsqrt(jnp.sum(pre * pre, axis=-1, keepdims=True) + 1e-06)
        unit = pre * inv_norm
        emb = unit.astype(jnp.bfloat16)

        rates = jnp.exp(label_log_rates)
        upper = (me // n_label) % 2
        place = jnp.stack([upper, me * label_rows]).astype(jnp.int32)
        keep, send, hits = label_pass(
            place, emb, label_matrix, rates[None, :], every[:, views * title :]
        )
        labeled_count = jnp.sum(all_labeled).astype(jnp.float32)
        batch_rate = hits[0] / labeled_count
        new_log_rates = jnp.log(0.9 * rates + 0.1 * batch_rate)

        summed = split_sum(keep, send, n, n_label)
        total = summed[docs, 0]
        loss_sum = summed[docs, 1]
        grad_emb = summed[:docs] * (16.0 / total)
        unit_strong = unit[docs:]
        grad_pre = (
            grad_emb - unit_strong * jnp.sum(unit_strong * grad_emb, axis=-1, keepdims=True)
        ) * inv_norm[docs:]
        grad_weight = jnp.einsum(
            "dk,dj->kj", pooled[docs:].astype(jnp.float32), grad_pre, precision=lax.Precision.HIGHEST
        )
        loss = loss_sum / total
        return (loss, grad_weight, new_log_rates)

    return shards


def solution(mesh):
    n = mesh.shape["dp"] * mesh.shape["label"]
    assert n & (n - 1) == 0, "n not pow2"
    return jax.shard_map(
        make_shards(n, mesh.shape["label"]),
        mesh=mesh,
        in_specs=(
            P(AXES, None, None),
            P(AXES),
            P(AXES, None),
            P(AXES, None),
            P(),
            P(AXES, None),
            P(AXES),
        ),
        out_specs=(P(), P(), P(AXES)),
        check_vma=False,
    )
```

```python
import functools

import jax
import jax.numpy as jnp
from jax import lax
from jax.experimental import pallas as pl
from jax.experimental.pallas import tpu as pltpu
from jax.sharding import PartitionSpec as P

AXES = ("dp", "label")


def tree_sum(x, n, n_label):
    me = lax.axis_index(AXES)
    upper = (me // n_label) % 2 == 1
    half = x.shape[1] // 2
    low, high = x[:, :half], x[:, half:]
    swap = [(i, i ^ n_label) for i in range(n)]
    x = jnp.where(upper, high, low) + lax.ppermute(jnp.where(upper, low, high), AXES, swap)
    rows = x.shape[0]
    part = lax.all_to_all(x.reshape(n_label, rows // n_label, half), "label", 0, 0, tiled=False)
    part = jnp.sum(part, axis=0)
    step = 2 * n_label
    while step < n:
        part = part + lax.ppermute(part, AXES, [(i, i ^ step) for i in range(n)])
        step *= 2
    every = jnp.broadcast_to(part[None], (n_label,) + part.shape)
    x = lax.all_to_all(every, "label", 0, 0, tiled=False).reshape(rows, half)
    other = lax.ppermute(x, AXES, swap)
    return jnp.where(upper, jnp.concatenate([other, x], 1), jnp.concatenate([x, other], 1))


def label_kernel(first, place_ref, emb_ref, lab_ref, rate_ref, ints_ref, keep_ref, send_ref, rate_out_ref):
    tile = pl.program_id(0)
    upper = place_ref[0] == 1
    base = place_ref[1]
    docs, half = send_ref.shape[0] - 8, send_ref.shape[1]
    width = lab_ref.shape[0]
    n_pos = ints_ref.shape[1] - 1 - first
    lab = lab_ref[...]
    scores = (
        lax.dot_general(emb_ref[...], lab, (((1,), (1,)), ((), ())), preferred_element_type=jnp.float32)
        * 16.0
        - 6.0
    )
    weak = scores[:docs]
    strong = scores[docs:]
    teacher = jax.nn.sigmoid(weak)
    mean_teacher = jnp.sum(teacher, axis=0, keepdims=True) / docs
    codes = base + tile * width + lax.broadcasted_iota(jnp.int32, (1, width), 1)
    ints = ints_ref[...]
    hit = ints[:, first : first + 1] == codes
    for column in range(first + 1, first + n_pos):
        hit = hit | (ints[:, column : column + 1] == codes)
    hit = hit.astype(jnp.float32)
    flag = (ints[:, first + n_pos : first + n_pos + 1] == 1).astype(jnp.float32)
    target = jnp.where(flag > 0.5, hit, teacher * jnp.exp(rate_ref[...]) / mean_teacher)
    softplus = jnp.maximum(strong, 0.0) + jnp.log1p(jnp.exp(-jnp.abs(strong)))
    slope = (jax.nn.sigmoid(strong) - target).astype(jnp.bfloat16)
    rate_out_ref[...] = jnp.sum(flag * hit, axis=0, keepdims=True)
    part = jnp.dot(slope, lab, preferred_element_type=jnp.float32)
    low, high = part[:, :half], part[:, half:]
    lane = lax.broadcasted_iota(jnp.int32, (8, half), 1)
    row = lax.broadcasted_iota(jnp.int32, (8, half), 0)
    total = jnp.sum(target)
    loss = jnp.sum(softplus - target * strong)
    extra = jnp.where(row == 0, jnp.where(lane == 0, total, jnp.where(lane == 1, loss, 0.0)), 0.0)
    keep = jnp.concatenate([jnp.where(upper, high, low), jnp.where(upper, 0.0, extra)], axis=0)
    send = jnp.concatenate([jnp.where(upper, low, high), jnp.where(upper, extra, 0.0)], axis=0)

    @pl.when(tile == 0)
    def _():
        keep_ref[...] = keep
        send_ref[...] = send

    @pl.when(tile > 0)
    def _():
        keep_ref[...] += keep
        send_ref[...] += send


def label_pass(place, emb, label_matrix, log_rates, ints, first):
    rows, depth = emb.shape
    docs = ints.shape[0]
    labels = label_matrix.shape[0]
    width = 1024 if labels % 1024 == 0 else labels
    half = depth // 2
    return pl.pallas_call(
        functools.partial(label_kernel, first),
        grid_spec=pltpu.PrefetchScalarGridSpec(
            num_scalar_prefetch=1,
            grid=(labels // width,),
            in_specs=[
                pl.BlockSpec((rows, depth), lambda i, p: (0, 0)),
                pl.BlockSpec((width, depth), lambda i, p: (i, 0)),
                pl.BlockSpec((1, width), lambda i, p: (0, i)),
                pl.BlockSpec(ints.shape, lambda i, p: (0, 0)),
            ],
            out_specs=[
                pl.BlockSpec((docs + 8, half), lambda i, p: (0, 0)),
                pl.BlockSpec((docs + 8, half), lambda i, p: (0, 0)),
                pl.BlockSpec((1, width), lambda i, p: (0, i)),
            ],
        ),
        out_shape=[
            jax.ShapeDtypeStruct((docs + 8, half), jnp.float32),
            jax.ShapeDtypeStruct((docs + 8, half), jnp.float32),
            jax.ShapeDtypeStruct((1, labels), jnp.float32),
        ],
        compiler_params=pltpu.CompilerParams(dimension_semantics=("arbitrary",)),
    )(place, emb, label_matrix, log_rates, ints)


def split_sum(keep, send, n, pair_step):
    me = lax.axis_index(AXES)
    upper = (me // pair_step) % 2 == 1
    swap = [(i, i ^ pair_step) for i in range(n)]
    x = keep + lax.ppermute(send, AXES, swap)
    step = 1
    while step < n:
        if step != pair_step:
            x = x + lax.ppermute(x, AXES, [(i, i ^ step) for i in range(n)])
        step *= 2
    other = lax.ppermute(x, AXES, swap)
    return jnp.where(upper, jnp.concatenate([other, x], 1), jnp.concatenate([x, other], 1))


def make_shards(n, n_label):
    def shards(
        token_ids, labeled, positive_ids, vocab_table, enc_weight, label_matrix, label_log_rates
    ):
        own_docs, views, title = token_ids.shape
        n_pos = positive_ids.shape[1]
        vocab_rows, width = vocab_table.shape
        label_rows = label_matrix.shape[0]
        me = lax.axis_index(AXES)
        docs = own_docs * n

        packed = jnp.concatenate(
            [token_ids.reshape(own_docs, views * title), positive_ids, labeled[:, None]], axis=1
        )
        spread = jnp.broadcast_to(packed[None], (n,) + packed.shape)
        every = lax.all_to_all(spread, AXES, 0, 0, tiled=False).reshape(docs, packed.shape[1])
        all_tokens = every[:, : views * title].reshape(docs, views, title)
        all_labeled = every[:, views * title + n_pos]

        rows = jnp.transpose(all_tokens, (1, 0, 2)).reshape(views * docs, title) - me * vocab_rows
        codes = jnp.arange(vocab_rows, dtype=jnp.int32)
        tally = jnp.zeros((views * docs, vocab_rows), jnp.float32)
        for position in range(title):
            tally = tally + (rows[:, position : position + 1] == codes[None, :]).astype(jnp.float32)
        partial = jnp.dot(tally.astype(jnp.bfloat16), vocab_table, preferred_element_type=jnp.float32)
        pooled = (tree_sum(partial, n, n_label) * (1.0 / title)).astype(jnp.bfloat16)

        pre = jnp.dot(pooled, enc_weight, preferred_element_type=jnp.float32)
        inv_norm = lax.rsqrt(jnp.sum(pre * pre, axis=-1, keepdims=True) + 1e-06)
        unit = pre * inv_norm
        emb = unit.astype(jnp.bfloat16)

        upper = (me // n_label) % 2
        place = jnp.stack([upper, me * label_rows]).astype(jnp.int32)
        keep, send, hits = label_pass(
            place, emb, label_matrix, label_log_rates[None, :], every, views * title
        )
        labeled_count = jnp.sum(all_labeled).astype(jnp.float32)
        batch_rate = hits[0] / labeled_count
        new_log_rates = jnp.log(0.9 * jnp.exp(label_log_rates) + 0.1 * batch_rate)

        summed = split_sum(keep, send, n, n_label)
        total = summed[docs, 0]
        loss_sum = summed[docs, 1]
        grad_emb = summed[:docs] * 16.0 / total
        unit_strong = unit[docs:]
        grad_pre = (
            grad_emb - unit_strong * jnp.sum(unit_strong * grad_emb, axis=-1, keepdims=True)
        ) * inv_norm[docs:]
        first_piece = lax.reduce_precision(grad_pre, exponent_bits=8, mantissa_bits=7)
        rest = grad_pre - first_piece
        second_piece = lax.reduce_precision(rest, exponent_bits=8, mantissa_bits=7)
        third_piece = rest - second_piece
        pieces = jnp.concatenate([first_piece, second_piece, third_piece], axis=0)
        pieces = pieces.astype(jnp.bfloat16)
        strong_pooled = jnp.concatenate([pooled[docs:]] * 3, axis=0)
        grad_weight = jnp.einsum(
            "dk,dj->kj", strong_pooled, pieces, preferred_element_type=jnp.float32
        )
        loss = loss_sum / total
        return (loss, grad_weight, new_log_rates)

    return shards


def solution(mesh):
    n = mesh.shape["dp"] * mesh.shape["label"]
    assert n & (n - 1) == 0, "n not pow2"
    return jax.shard_map(
        make_shards(n, mesh.shape["label"]),
        mesh=mesh,
        in_specs=(
            P(AXES, None, None),
            P(AXES),
            P(AXES, None),
            P(AXES, None),
            P(),
            P(AXES, None),
            P(AXES),
        ),
        out_specs=(P(), P(), P(AXES)),
        check_vma=False,
    )
```

```python
import functools

import jax
import jax.numpy as jnp
from jax import lax
from jax.experimental import pallas as pl
from jax.experimental.pallas import tpu as pltpu
from jax.sharding import PartitionSpec as P

AXES = ("dp", "label")


def tree_sum(x, n, n_label):
    me = lax.axis_index(AXES)
    upper = (me // n_label) % 2 == 1
    half = x.shape[1] // 2
    low, high = x[:, :half], x[:, half:]
    swap = [(i, i ^ n_label) for i in range(n)]
    x = jnp.where(upper, high, low) + lax.ppermute(jnp.where(upper, low, high), AXES, swap)
    rows = x.shape[0]
    part = lax.all_to_all(x.reshape(n_label, rows // n_label, half), "label", 0, 0, tiled=False)
    part = jnp.sum(part, axis=0)
    step = 2 * n_label
    while step < n:
        part = part + lax.ppermute(part, AXES, [(i, i ^ step) for i in range(n)])
        step *= 2
    every = jnp.broadcast_to(part[None], (n_label,) + part.shape)
    x = lax.all_to_all(every, "label", 0, 0, tiled=False).reshape(rows, half)
    other = lax.ppermute(x, AXES, swap)
    return jnp.where(upper, jnp.concatenate([other, x], 1), jnp.concatenate([x, other], 1))


def label_kernel(first, n_pos, place_ref, emb_ref, lab_ref, rate_ref, ints_ref, keep_ref, send_ref, rate_out_ref):
    tile = pl.program_id(0)
    upper = place_ref[0] == 1
    base = place_ref[1]
    docs, half = send_ref.shape[0] - 8, send_ref.shape[1]
    width = lab_ref.shape[0]
    lab = lab_ref[...]
    scores = (
        lax.dot_general(emb_ref[...], lab, (((1,), (1,)), ((), ())), preferred_element_type=jnp.float32)
        * 16.0
        - 6.0
    )
    weak = scores[:docs]
    strong = scores[docs:]
    teacher = jax.nn.sigmoid(weak)
    mean_teacher = jnp.sum(teacher, axis=0, keepdims=True) / docs
    codes = base + tile * width + lax.broadcasted_iota(jnp.int32, (1, width), 1)
    ints = ints_ref[...]
    hit = ints[:, first : first + 1] == codes
    for column in range(first + 1, first + n_pos):
        hit = hit | (ints[:, column : column + 1] == codes)
    hit = hit.astype(jnp.float32)
    flag = (ints[:, first + n_pos : first + n_pos + 1] == 1).astype(jnp.float32)
    target = jnp.where(flag > 0.5, hit, teacher * jnp.exp(rate_ref[...]) / mean_teacher)
    softplus = jnp.maximum(strong, 0.0) + jnp.log1p(jnp.exp(-jnp.abs(strong)))
    slope = (jax.nn.sigmoid(strong) - target).astype(jnp.bfloat16)
    rate_out_ref[...] = jnp.sum(flag * hit, axis=0, keepdims=True)
    part = jnp.dot(slope, lab, preferred_element_type=jnp.float32)
    low, high = part[:, :half], part[:, half:]
    lane = lax.broadcasted_iota(jnp.int32, (8, half), 1)
    row = lax.broadcasted_iota(jnp.int32, (8, half), 0)
    total = jnp.sum(target)
    loss = jnp.sum(softplus - target * strong)
    extra = jnp.where(row == 0, jnp.where(lane == 0, total, jnp.where(lane == 1, loss, 0.0)), 0.0)
    keep = jnp.concatenate([jnp.where(upper, high, low), jnp.where(upper, 0.0, extra)], axis=0)
    send = jnp.concatenate([jnp.where(upper, low, high), jnp.where(upper, extra, 0.0)], axis=0)

    @pl.when(tile == 0)
    def _():
        keep_ref[...] = keep
        send_ref[...] = send

    @pl.when(tile > 0)
    def _():
        keep_ref[...] += keep
        send_ref[...] += send


def label_pass(place, emb, label_matrix, log_rates, ints, first, n_pos):
    rows, depth = emb.shape
    docs = ints.shape[0]
    labels = label_matrix.shape[0]
    width = 1024 if labels % 1024 == 0 else labels
    half = depth // 2
    return pl.pallas_call(
        functools.partial(label_kernel, first, n_pos),
        grid_spec=pltpu.PrefetchScalarGridSpec(
            num_scalar_prefetch=1,
            grid=(labels // width,),
            in_specs=[
                pl.BlockSpec((rows, depth), lambda i, p: (0, 0)),
                pl.BlockSpec((width, depth), lambda i, p: (i, 0)),
                pl.BlockSpec((1, width), lambda i, p: (0, i)),
                pl.BlockSpec(ints.shape, lambda i, p: (0, 0)),
            ],
            out_specs=[
                pl.BlockSpec((docs + 8, half), lambda i, p: (0, 0)),
                pl.BlockSpec((docs + 8, half), lambda i, p: (0, 0)),
                pl.BlockSpec((1, width), lambda i, p: (0, i)),
            ],
        ),
        out_shape=[
            jax.ShapeDtypeStruct((docs + 8, half), jnp.float32),
            jax.ShapeDtypeStruct((docs + 8, half), jnp.float32),
            jax.ShapeDtypeStruct((1, labels), jnp.float32),
        ],
        compiler_params=pltpu.CompilerParams(dimension_semantics=("arbitrary",)),
    )(place, emb, label_matrix, log_rates, ints)


def split_sum(keep, send, n, pair_step):
    me = lax.axis_index(AXES)
    upper = (me // pair_step) % 2 == 1
    swap = [(i, i ^ pair_step) for i in range(n)]
    x = keep + lax.ppermute(send, AXES, swap)
    step = 1
    while step < n:
        if step != pair_step:
            x = x + lax.ppermute(x, AXES, [(i, i ^ step) for i in range(n)])
        step *= 2
    other = lax.ppermute(x, AXES, swap)
    return jnp.where(upper, jnp.concatenate([other, x], 1), jnp.concatenate([x, other], 1))


def make_shards(n, n_label):
    def shards(
        token_ids, labeled, positive_ids, vocab_table, enc_weight, label_matrix, label_log_rates
    ):
        own_docs, views, title = token_ids.shape
        n_pos = positive_ids.shape[1]
        vocab_rows, width = vocab_table.shape
        label_rows = label_matrix.shape[0]
        me = lax.axis_index(AXES)
        docs = own_docs * n

        side = jnp.concatenate(
            [positive_ids, labeled[:, None], jnp.zeros((own_docs, title - n_pos - 1), jnp.int32)], axis=1
        )
        packed = jnp.concatenate([token_ids, side[:, None, :]], axis=1)
        spread = jnp.broadcast_to(packed[None], (n,) + packed.shape)
        every = lax.all_to_all(spread, AXES, 0, 0, tiled=False).reshape(docs, views + 1, title)
        all_tokens = every[:, :views]
        side_all = every[:, views]
        all_labeled = side_all[:, n_pos]

        rows = jnp.transpose(all_tokens, (1, 0, 2)).reshape(views * docs, title) - me * vocab_rows
        codes = jnp.arange(vocab_rows, dtype=jnp.int32)
        tally = jnp.zeros((views * docs, vocab_rows), jnp.float32)
        for position in range(title):
            tally = tally + (rows[:, position : position + 1] == codes[None, :]).astype(jnp.float32)
        partial = jnp.dot(tally.astype(jnp.bfloat16), vocab_table, preferred_element_type=jnp.float32)
        pooled = (tree_sum(partial, n, n_label) * (1.0 / title)).astype(jnp.bfloat16)

        pre = jnp.dot(pooled, enc_weight, preferred_element_type=jnp.float32)
        inv_norm = lax.rsqrt(jnp.sum(pre * pre, axis=-1, keepdims=True) + 1e-06)
        unit = pre * inv_norm
        emb = unit.astype(jnp.bfloat16)

        upper = (me // n_label) % 2
        place = jnp.stack([upper, me * label_rows]).astype(jnp.int32)
        keep, send, hits = label_pass(
            place, emb, label_matrix, label_log_rates[None, :], side_all, 0, n_pos
        )
        labeled_count = jnp.sum(all_labeled).astype(jnp.float32)
        batch_rate = hits[0] / labeled_count
        new_log_rates = jnp.log(0.9 * jnp.exp(label_log_rates) + 0.1 * batch_rate)

        summed = split_sum(keep, send, n, n_label)
        total = summed[docs, 0]
        grad_emb = summed[:docs] * 16.0 / total
        unit_strong = unit[docs:]
        grad_pre = (
            grad_emb - unit_strong * jnp.sum(unit_strong * grad_emb, axis=-1, keepdims=True)
        ) * inv_norm[docs:]
        first_piece = lax.reduce_precision(grad_pre, exponent_bits=8, mantissa_bits=7)
        rest = grad_pre - first_piece
        second_piece = lax.reduce_precision(rest, exponent_bits=8, mantissa_bits=7)
        third_piece = rest - second_piece
        pieces = jnp.concatenate([first_piece, second_piece, third_piece], axis=0)
        pieces = pieces.astype(jnp.bfloat16)
        strong_pooled = jnp.concatenate([pooled[docs:]] * 3, axis=0)
        grad_weight = jnp.einsum(
            "dk,dj->kj", strong_pooled, pieces, preferred_element_type=jnp.float32
        )
        loss = jnp.reshape(summed[docs : docs + 1, 1:2] / summed[docs : docs + 1, 0:1], ())
        return (loss, grad_weight, new_log_rates)

    return shards


def solution(mesh):
    n = mesh.shape["dp"] * mesh.shape["label"]
    assert n & (n - 1) == 0, "n not pow2"
    return jax.shard_map(
        make_shards(n, mesh.shape["label"]),
        mesh=mesh,
        in_specs=(
            P(AXES, None, None),
            P(AXES),
            P(AXES, None),
            P(AXES, None),
            P(),
            P(AXES, None),
            P(AXES),
        ),
        out_specs=(P(), P(), P(AXES)),
        check_vma=False,
    )
```

```python
import functools

import jax
import jax.numpy as jnp
from jax import lax
from jax.experimental import pallas as pl
from jax.experimental.pallas import tpu as pltpu
from jax.sharding import PartitionSpec as P

AXES = ("dp", "label")


def tree_sum(x, n, n_label):
    me = lax.axis_index(AXES)
    upper = (me // n_label) % 2 == 1
    half = x.shape[1] // 2
    low, high = x[:, :half], x[:, half:]
    swap = [(i, i ^ n_label) for i in range(n)]
    x = jnp.where(upper, high, low) + lax.ppermute(jnp.where(upper, low, high), AXES, swap)
    rows = x.shape[0]
    part = lax.all_to_all(x.reshape(n_label, rows // n_label, half), "label", 0, 0, tiled=False)
    part = jnp.sum(part, axis=0)
    step = 2 * n_label
    while step < n:
        part = part + lax.ppermute(part, AXES, [(i, i ^ step) for i in range(n)])
        step *= 2
    every = jnp.broadcast_to(part[None], (n_label,) + part.shape)
    x = lax.all_to_all(every, "label", 0, 0, tiled=False).reshape(rows, half)
    other = lax.ppermute(x, AXES, swap)
    return jnp.where(upper, jnp.concatenate([other, x], 1), jnp.concatenate([x, other], 1))


def label_kernel(first, place_ref, emb_ref, lab_ref, rate_ref, ints_ref, keep_ref, send_ref, rate_out_ref):
    tile = pl.program_id(0)
    upper = place_ref[0] == 1
    base = place_ref[1]
    docs, half = send_ref.shape[0] - 8, send_ref.shape[1]
    width = lab_ref.shape[0]
    n_pos = ints_ref.shape[1] - 1 - first
    lab = lab_ref[...]
    scores = (
        lax.dot_general(emb_ref[...], lab, (((1,), (1,)), ((), ())), preferred_element_type=jnp.float32)
        * 16.0
        - 6.0
    )
    weak = scores[:docs]
    strong = scores[docs:]
    teacher = jax.nn.sigmoid(weak)
    mean_teacher = jnp.sum(teacher, axis=0, keepdims=True) / docs
    codes = base + tile * width + lax.broadcasted_iota(jnp.int32, (1, width), 1)
    ints = ints_ref[...]
    hit = ints[:, first : first + 1] == codes
    for column in range(first + 1, first + n_pos):
        hit = hit | (ints[:, column : column + 1] == codes)
    hit = hit.astype(jnp.float32)
    flag = (ints[:, first + n_pos : first + n_pos + 1] == 1).astype(jnp.float32)
    target = jnp.where(flag > 0.5, hit, teacher * jnp.exp(rate_ref[...]) / mean_teacher)
    softplus = jnp.maximum(strong, 0.0) + jnp.log1p(jnp.exp(-jnp.abs(strong)))
    slope = (jax.nn.sigmoid(strong) - target).astype(jnp.bfloat16)
    rate_out_ref[...] = jnp.sum(flag * hit, axis=0, keepdims=True)
    part = jnp.dot(slope, lab, preferred_element_type=jnp.float32)
    low, high = part[:, :half], part[:, half:]
    lane = lax.broadcasted_iota(jnp.int32, (8, half), 1)
    row = lax.broadcasted_iota(jnp.int32, (8, half), 0)
    total = jnp.sum(target)
    loss = jnp.sum(softplus - target * strong)
    extra = jnp.where(row == 0, jnp.where(lane == 0, total, jnp.where(lane == 1, loss, 0.0)), 0.0)
    keep = jnp.concatenate([jnp.where(upper, high, low), jnp.where(upper, 0.0, extra)], axis=0)
    send = jnp.concatenate([jnp.where(upper, low, high), jnp.where(upper, extra, 0.0)], axis=0)

    @pl.when(tile == 0)
    def _():
        keep_ref[...] = keep
        send_ref[...] = send

    @pl.when(tile > 0)
    def _():
        keep_ref[...] += keep
        send_ref[...] += send


def label_pass(place, emb, label_matrix, log_rates, ints, first):
    rows, depth = emb.shape
    docs = ints.shape[0]
    labels = label_matrix.shape[0]
    width = 1024 if labels % 1024 == 0 else labels
    half = depth // 2
    return pl.pallas_call(
        functools.partial(label_kernel, first),
        grid_spec=pltpu.PrefetchScalarGridSpec(
            num_scalar_prefetch=1,
            grid=(labels // width,),
            in_specs=[
                pl.BlockSpec((rows, depth), lambda i, p: (0, 0)),
                pl.BlockSpec((width, depth), lambda i, p: (i, 0)),
                pl.BlockSpec((1, width), lambda i, p: (0, i)),
                pl.BlockSpec(ints.shape, lambda i, p: (0, 0)),
            ],
            out_specs=[
                pl.BlockSpec((docs + 8, half), lambda i, p: (0, 0)),
                pl.BlockSpec((docs + 8, half), lambda i, p: (0, 0)),
                pl.BlockSpec((1, width), lambda i, p: (0, i)),
            ],
        ),
        out_shape=[
            jax.ShapeDtypeStruct((docs + 8, half), jnp.float32),
            jax.ShapeDtypeStruct((docs + 8, half), jnp.float32),
            jax.ShapeDtypeStruct((1, labels), jnp.float32),
        ],
        compiler_params=pltpu.CompilerParams(dimension_semantics=("arbitrary",)),
    )(place, emb, label_matrix, log_rates, ints)


def tail_kernel(upper_ref, mine_ref, other_ref, unit_ref, inv_ref, pooled_t_ref, weight_ref, loss_ref):
    upper = upper_ref[0] == 1
    docs = unit_ref.shape[0]
    half = mine_ref.shape[1]
    mine = mine_ref[...]
    other = other_ref[...]
    low = jnp.where(upper, other, mine)
    high = jnp.where(upper, mine, other)
    total = low[docs : docs + 1, 0:1]
    loss_ref[...] = low[docs : docs + 1, 1:2] / total
    unit = unit_ref[...]
    grad_low = low[:docs] * 16.0 / total
    grad_high = high[:docs] * 16.0 / total
    along = jnp.sum(unit[:, :half] * grad_low, axis=1, keepdims=True) + jnp.sum(
        unit[:, half:] * grad_high, axis=1, keepdims=True
    )
    inv = inv_ref[...]
    pooled_t = pooled_t_ref[...]
    for index, grad in enumerate((grad_low, grad_high)):
        pre = (grad - unit[:, index * half : (index + 1) * half] * along) * inv
        first = pre.astype(jnp.bfloat16)
        rest = pre - first.astype(jnp.float32)
        second = rest.astype(jnp.bfloat16)
        third = (rest - second.astype(jnp.float32)).astype(jnp.bfloat16)
        acc = jnp.dot(pooled_t, first, preferred_element_type=jnp.float32)
        acc = acc + jnp.dot(pooled_t, second, preferred_element_type=jnp.float32)
        acc = acc + jnp.dot(pooled_t, third, preferred_element_type=jnp.float32)
        weight_ref[:, index * half : (index + 1) * half] = acc


def tail_pass(upper, mine, other, unit, inv, pooled_t):
    depth = pooled_t.shape[0]
    vmem = pltpu.MemorySpace.VMEM
    return pl.pallas_call(
        tail_kernel,
        in_specs=[pl.BlockSpec(memory_space=pltpu.MemorySpace.SMEM)] + [pl.BlockSpec(memory_space=vmem)] * 5,
        out_specs=[pl.BlockSpec(memory_space=vmem), pl.BlockSpec(memory_space=vmem)],
        out_shape=[
            jax.ShapeDtypeStruct((depth, depth), jnp.float32),
            jax.ShapeDtypeStruct((1, 1), jnp.float32),
        ],
    )(upper, mine, other, unit, inv, pooled_t)


def split_sum(keep, send, n, pair_step):
    swap = [(i, i ^ pair_step) for i in range(n)]
    x = keep + lax.ppermute(send, AXES, swap)
    step = 1
    while step < n:
        if step != pair_step:
            x = x + lax.ppermute(x, AXES, [(i, i ^ step) for i in range(n)])
        step *= 2
    return x, lax.ppermute(x, AXES, swap)


def make_shards(n, n_label):
    def shards(
        token_ids, labeled, positive_ids, vocab_table, enc_weight, label_matrix, label_log_rates
    ):
        own_docs, views, title = token_ids.shape
        n_pos = positive_ids.shape[1]
        vocab_rows, width = vocab_table.shape
        label_rows = label_matrix.shape[0]
        me = lax.axis_index(AXES)
        docs = own_docs * n

        packed = jnp.concatenate(
            [token_ids.reshape(own_docs, views * title), positive_ids, labeled[:, None]], axis=1
        )
        spread = jnp.broadcast_to(packed[None], (n,) + packed.shape)
        every = lax.all_to_all(spread, AXES, 0, 0, tiled=False).reshape(docs, packed.shape[1])
        all_tokens = every[:, : views * title].reshape(docs, views, title)
        all_labeled = every[:, views * title + n_pos]

        rows = jnp.transpose(all_tokens, (1, 0, 2)).reshape(views * docs, title) - me * vocab_rows
        codes = jnp.arange(vocab_rows, dtype=jnp.int32)
        tally = jnp.zeros((views * docs, vocab_rows), jnp.float32)
        for position in range(title):
            tally = tally + (rows[:, position : position + 1] == codes[None, :]).astype(jnp.float32)
        partial = jnp.dot(tally.astype(jnp.bfloat16), vocab_table, preferred_element_type=jnp.float32)
        pooled = (tree_sum(partial, n, n_label) * (1.0 / title)).astype(jnp.bfloat16)

        pre = jnp.dot(pooled, enc_weight, preferred_element_type=jnp.float32)
        inv_norm = lax.rsqrt(jnp.sum(pre * pre, axis=-1, keepdims=True) + 1e-06)
        unit = pre * inv_norm
        emb = unit.astype(jnp.bfloat16)

        upper = (me // n_label) % 2
        place = jnp.stack([upper, me * label_rows]).astype(jnp.int32)
        keep, send, hits = label_pass(
            place, emb, label_matrix, label_log_rates[None, :], every, views * title
        )
        labeled_count = jnp.sum(all_labeled).astype(jnp.float32)
        batch_rate = hits[0] / labeled_count
        new_log_rates = jnp.log(0.9 * jnp.exp(label_log_rates) + 0.1 * batch_rate)

        mine, other = split_sum(keep, send, n, n_label)
        grad_weight, loss = tail_pass(
            upper.astype(jnp.int32)[None], mine, other, unit[docs:], inv_norm[docs:], pooled[docs:].T
        )
        loss = loss.reshape(())
        return (loss, grad_weight, new_log_rates)

    return shards


def solution(mesh):
    n = mesh.shape["dp"] * mesh.shape["label"]
    assert n & (n - 1) == 0, "n not pow2"
    return jax.shard_map(
        make_shards(n, mesh.shape["label"]),
        mesh=mesh,
        in_specs=(
            P(AXES, None, None),
            P(AXES),
            P(AXES, None),
            P(AXES, None),
            P(),
            P(AXES, None),
            P(AXES),
        ),
        out_specs=(P(), P(), P(AXES)),
        check_vma=False,
    )
```

```python
import functools

import jax
import jax.numpy as jnp
from jax import lax
from jax.experimental import pallas as pl
from jax.experimental.pallas import tpu as pltpu
from jax.sharding import PartitionSpec as P

AXES = ("dp", "label")


def tree_sum(x, n, n_label):
    me = lax.axis_index(AXES)
    upper = (me // n_label) % 2 == 1
    half = x.shape[1] // 2
    low, high = x[:, :half], x[:, half:]
    swap = [(i, i ^ n_label) for i in range(n)]
    x = jnp.where(upper, high, low) + lax.ppermute(jnp.where(upper, low, high), AXES, swap)
    rows = x.shape[0]
    part = lax.all_to_all(x.reshape(n_label, rows // n_label, half), "label", 0, 0, tiled=False)
    part = jnp.sum(part, axis=0)
    step = 2 * n_label
    while step < n:
        part = part + lax.ppermute(part, AXES, [(i, i ^ step) for i in range(n)])
        step *= 2
    every = jnp.broadcast_to(part[None], (n_label,) + part.shape)
    x = lax.all_to_all(every, "label", 0, 0, tiled=False).reshape(rows, half)
    other = lax.ppermute(x, AXES, swap)
    return jnp.where(upper, jnp.concatenate([other, x], 1), jnp.concatenate([x, other], 1))


def label_kernel(first, place_ref, emb_ref, lab_ref, rate_ref, ints_ref, keep_ref, send_ref, rate_out_ref):
    tile = pl.program_id(0)
    upper = place_ref[0] == 1
    base = place_ref[1]
    docs, half = send_ref.shape[0] - 8, send_ref.shape[1]
    width = lab_ref.shape[0]
    n_pos = ints_ref.shape[1] - 1 - first
    lab = lab_ref[...]
    scores = (
        lax.dot_general(emb_ref[...], lab, (((1,), (1,)), ((), ())), preferred_element_type=jnp.float32)
        * 16.0
        - 6.0
    )
    weak = scores[:docs]
    strong = scores[docs:]
    teacher = jax.nn.sigmoid(weak)
    mean_teacher = jnp.sum(teacher, axis=0, keepdims=True) / docs
    codes = base + tile * width + lax.broadcasted_iota(jnp.int32, (1, width), 1)
    ints = ints_ref[...]
    hit = ints[:, first : first + 1] == codes
    for column in range(first + 1, first + n_pos):
        hit = hit | (ints[:, column : column + 1] == codes)
    hit = hit.astype(jnp.float32)
    flag = (ints[:, first + n_pos : first + n_pos + 1] == 1).astype(jnp.float32)
    target = jnp.where(flag > 0.5, hit, teacher * jnp.exp(rate_ref[...]) / mean_teacher)
    softplus = jnp.maximum(strong, 0.0) + jnp.log1p(jnp.exp(-jnp.abs(strong)))
    slope = (jax.nn.sigmoid(strong) - target).astype(jnp.bfloat16)
    rate_out_ref[...] = jnp.sum(flag * hit, axis=0, keepdims=True)
    part = jnp.dot(slope, lab, preferred_element_type=jnp.float32)
    low, high = part[:, :half], part[:, half:]
    lane = lax.broadcasted_iota(jnp.int32, (8, half), 1)
    row = lax.broadcasted_iota(jnp.int32, (8, half), 0)
    total = jnp.sum(target)
    loss = jnp.sum(softplus - target * strong)
    extra = jnp.where(row == 0, jnp.where(lane == 0, total, jnp.where(lane == 1, loss, 0.0)), 0.0)
    keep = jnp.concatenate([jnp.where(upper, high, low), jnp.where(upper, 0.0, extra)], axis=0)
    send = jnp.concatenate([jnp.where(upper, low, high), jnp.where(upper, extra, 0.0)], axis=0)

    @pl.when(tile == 0)
    def _():
        keep_ref[...] = keep
        send_ref[...] = send

    @pl.when(tile > 0)
    def _():
        keep_ref[...] += keep
        send_ref[...] += send


def label_pass(place, emb, label_matrix, log_rates, ints, first):
    rows, depth = emb.shape
    docs = ints.shape[0]
    labels = label_matrix.shape[0]
    width = 1024 if labels % 1024 == 0 else labels
    half = depth // 2
    return pl.pallas_call(
        functools.partial(label_kernel, first),
        grid_spec=pltpu.PrefetchScalarGridSpec(
            num_scalar_prefetch=1,
            grid=(labels // width,),
            in_specs=[
                pl.BlockSpec((rows, depth), lambda i, p: (0, 0)),
                pl.BlockSpec((width, depth), lambda i, p: (i, 0)),
                pl.BlockSpec((1, width), lambda i, p: (0, i)),
                pl.BlockSpec(ints.shape, lambda i, p: (0, 0)),
            ],
            out_specs=[
                pl.BlockSpec((docs + 8, half), lambda i, p: (0, 0)),
                pl.BlockSpec((docs + 8, half), lambda i, p: (0, 0)),
                pl.BlockSpec((1, width), lambda i, p: (0, i)),
            ],
        ),
        out_shape=[
            jax.ShapeDtypeStruct((docs + 8, half), jnp.float32),
            jax.ShapeDtypeStruct((docs + 8, half), jnp.float32),
            jax.ShapeDtypeStruct((1, labels), jnp.float32),
        ],
        compiler_params=pltpu.CompilerParams(dimension_semantics=("arbitrary",)),
    )(place, emb, label_matrix, log_rates, ints)


def tail_kernel(upper_ref, mine_ref, other_ref, unit_ref, inv_ref, pooled_t_ref, weight_ref, loss_ref):
    upper = upper_ref[0] == 1
    docs = pooled_t_ref.shape[1]
    half = mine_ref.shape[1]
    mine = mine_ref[...]
    other = other_ref[...]
    low = jnp.where(upper, other, mine)
    high = jnp.where(upper, mine, other)
    total = low[docs : docs + 1, 0:1]
    loss_ref[...] = low[docs : docs + 1, 1:2] / total
    unit = unit_ref[docs:, :]
    grad_low = low[:docs] * 16.0 / total
    grad_high = high[:docs] * 16.0 / total
    along = jnp.sum(unit[:, :half] * grad_low, axis=1, keepdims=True) + jnp.sum(
        unit[:, half:] * grad_high, axis=1, keepdims=True
    )
    inv = inv_ref[docs:, :]
    pooled_t = pooled_t_ref[...]
    for index, grad in enumerate((grad_low, grad_high)):
        pre = (grad - unit[:, index * half : (index + 1) * half] * along) * inv
        first = pre.astype(jnp.bfloat16)
        rest = pre - first.astype(jnp.float32)
        second = rest.astype(jnp.bfloat16)
        third = (rest - second.astype(jnp.float32)).astype(jnp.bfloat16)
        acc = jnp.dot(pooled_t, first, preferred_element_type=jnp.float32)
        acc = acc + jnp.dot(pooled_t, second, preferred_element_type=jnp.float32)
        acc = acc + jnp.dot(pooled_t, third, preferred_element_type=jnp.float32)
        weight_ref[:, index * half : (index + 1) * half] = acc


def tail_pass(upper, mine, other, unit, inv, pooled_t):
    depth = pooled_t.shape[0]
    vmem = pltpu.MemorySpace.VMEM
    return pl.pallas_call(
        tail_kernel,
        in_specs=[pl.BlockSpec(memory_space=pltpu.MemorySpace.SMEM)] + [pl.BlockSpec(memory_space=vmem)] * 5,
        out_specs=[pl.BlockSpec(memory_space=vmem), pl.BlockSpec(memory_space=vmem)],
        out_shape=[
            jax.ShapeDtypeStruct((depth, depth), jnp.float32),
            jax.ShapeDtypeStruct((1, 1), jnp.float32),
        ],
    )(upper, mine, other, unit, inv, pooled_t)


def split_sum(keep, send, n, pair_step):
    swap = [(i, i ^ pair_step) for i in range(n)]
    x = keep + lax.ppermute(send, AXES, swap)
    step = 1
    while step < n:
        if step != pair_step:
            x = x + lax.ppermute(x, AXES, [(i, i ^ step) for i in range(n)])
        step *= 2
    return x, lax.ppermute(x, AXES, swap)


def make_shards(n, n_label):
    def shards(
        token_ids, labeled, positive_ids, vocab_table, enc_weight, label_matrix, label_log_rates
    ):
        own_docs, views, title = token_ids.shape
        n_pos = positive_ids.shape[1]
        vocab_rows, width = vocab_table.shape
        label_rows = label_matrix.shape[0]
        me = lax.axis_index(AXES)
        docs = own_docs * n

        packed = jnp.concatenate(
            [token_ids.reshape(own_docs, views * title), positive_ids, labeled[:, None]], axis=1
        )
        spread = jnp.broadcast_to(packed[None], (n,) + packed.shape)
        every = lax.all_to_all(spread, AXES, 0, 0, tiled=False).reshape(docs, packed.shape[1])
        all_tokens = every[:, : views * title].reshape(docs, views, title)
        all_labeled = every[:, views * title + n_pos]

        rows = jnp.transpose(all_tokens, (1, 0, 2)).reshape(views * docs, title) - me * vocab_rows
        codes = jnp.arange(vocab_rows, dtype=jnp.int32)
        tally = jnp.zeros((views * docs, vocab_rows), jnp.float32)
        for position in range(title):
            tally = tally + (rows[:, position : position + 1] == codes[None, :]).astype(jnp.float32)
        partial = jnp.dot(tally.astype(jnp.bfloat16), vocab_table, preferred_element_type=jnp.float32)
        pooled = (tree_sum(partial, n, n_label) * (1.0 / title)).astype(jnp.bfloat16)

        pre = jnp.dot(pooled, enc_weight, preferred_element_type=jnp.float32)
        inv_norm = lax.rsqrt(jnp.sum(pre * pre, axis=-1, keepdims=True) + 1e-06)
        unit = pre * inv_norm
        emb = unit.astype(jnp.bfloat16)

        upper = (me // n_label) % 2
        place = jnp.stack([upper, me * label_rows]).astype(jnp.int32)
        keep, send, hits = label_pass(
            place, emb, label_matrix, label_log_rates[None, :], every, views * title
        )
        labeled_count = jnp.sum(all_labeled).astype(jnp.float32)
        batch_rate = hits[0] / labeled_count
        new_log_rates = jnp.log(0.9 * jnp.exp(label_log_rates) + 0.1 * batch_rate)

        mine, other = split_sum(keep, send, n, n_label)
        grad_weight, loss = tail_pass(
            upper.astype(jnp.int32)[None], mine, other, unit, inv_norm, pooled[docs:].T
        )
        loss = loss.reshape(())
        return (loss, grad_weight, new_log_rates)

    return shards


def solution(mesh):
    n = mesh.shape["dp"] * mesh.shape["label"]
    assert n & (n - 1) == 0, "n not pow2"
    return jax.shard_map(
        make_shards(n, mesh.shape["label"]),
        mesh=mesh,
        in_specs=(
            P(AXES, None, None),
            P(AXES),
            P(AXES, None),
            P(AXES, None),
            P(),
            P(AXES, None),
            P(AXES),
        ),
        out_specs=(P(), P(), P(AXES)),
        check_vma=False,
    )
```

```python
import functools

import jax
import jax.numpy as jnp
from jax import lax
from jax.experimental import pallas as pl
from jax.experimental.pallas import tpu as pltpu
from jax.sharding import PartitionSpec as P

AXES = ("dp", "label")


def tree_sum(x, n, n_label):
    me = lax.axis_index(AXES)
    upper = (me // n_label) % 2 == 1
    half = x.shape[1] // 2
    low, high = x[:, :half], x[:, half:]
    swap = [(i, i ^ n_label) for i in range(n)]
    x = jnp.where(upper, high, low) + lax.ppermute(jnp.where(upper, low, high), AXES, swap)
    rows = x.shape[0]
    part = lax.all_to_all(x.reshape(n_label, rows // n_label, half), "label", 0, 0, tiled=False)
    part = jnp.sum(part, axis=0)
    step = 2 * n_label
    while step < n:
        part = part + lax.ppermute(part, AXES, [(i, i ^ step) for i in range(n)])
        step *= 2
    every = jnp.broadcast_to(part[None], (n_label,) + part.shape)
    x = lax.all_to_all(every, "label", 0, 0, tiled=False).reshape(rows, half)
    other = lax.ppermute(x, AXES, swap)
    return jnp.where(upper, jnp.concatenate([other, x], 1), jnp.concatenate([x, other], 1))


def label_kernel(first, place_ref, emb_ref, lab_ref, rate_ref, ints_ref, keep_ref, send_ref, rate_out_ref):
    tile = pl.program_id(0)
    upper = place_ref[0] == 1
    base = place_ref[1]
    docs, half = send_ref.shape[0] - 8, send_ref.shape[1]
    width = lab_ref.shape[0]
    n_pos = ints_ref.shape[1] - 1 - first
    lab = lab_ref[...]
    scores = (
        lax.dot_general(emb_ref[...], lab, (((1,), (1,)), ((), ())), preferred_element_type=jnp.float32)
        * 16.0
        - 6.0
    )
    weak = scores[:docs]
    strong = scores[docs:]
    teacher = jax.nn.sigmoid(weak)
    mean_teacher = jnp.sum(teacher, axis=0, keepdims=True) / docs
    codes = base + tile * width + lax.broadcasted_iota(jnp.int32, (1, width), 1)
    ints = ints_ref[...]
    hit = ints[:, first : first + 1] == codes
    for column in range(first + 1, first + n_pos):
        hit = hit | (ints[:, column : column + 1] == codes)
    hit = hit.astype(jnp.float32)
    flag = (ints[:, first + n_pos : first + n_pos + 1] == 1).astype(jnp.float32)
    target = jnp.where(flag > 0.5, hit, teacher * jnp.exp(rate_ref[...]) / mean_teacher)
    softplus = jnp.maximum(strong, 0.0) + jnp.log1p(jnp.exp(-jnp.abs(strong)))
    slope = (jax.nn.sigmoid(strong) - target).astype(jnp.bfloat16)
    count = jnp.sum(ints[:, first + n_pos : first + n_pos + 1].astype(jnp.float32))
    batch_rate = jnp.sum(flag * hit, axis=0, keepdims=True) / count
    rate_out_ref[...] = jnp.log(0.9 * jnp.exp(rate_ref[...]) + 0.1 * batch_rate)
    part = jnp.dot(slope, lab, preferred_element_type=jnp.float32)
    low, high = part[:, :half], part[:, half:]
    lane = lax.broadcasted_iota(jnp.int32, (8, half), 1)
    row = lax.broadcasted_iota(jnp.int32, (8, half), 0)
    total = jnp.sum(target)
    loss = jnp.sum(softplus - target * strong)
    extra = jnp.where(row == 0, jnp.where(lane == 0, total, jnp.where(lane == 1, loss, 0.0)), 0.0)
    keep = jnp.concatenate([jnp.where(upper, high, low), jnp.where(upper, 0.0, extra)], axis=0)
    send = jnp.concatenate([jnp.where(upper, low, high), jnp.where(upper, extra, 0.0)], axis=0)

    @pl.when(tile == 0)
    def _():
        keep_ref[...] = keep
        send_ref[...] = send

    @pl.when(tile > 0)
    def _():
        keep_ref[...] += keep
        send_ref[...] += send


def label_pass(place, emb, label_matrix, log_rates, ints, first):
    rows, depth = emb.shape
    docs = ints.shape[0]
    labels = label_matrix.shape[0]
    width = 1024 if labels % 1024 == 0 else labels
    half = depth // 2
    return pl.pallas_call(
        functools.partial(label_kernel, first),
        grid_spec=pltpu.PrefetchScalarGridSpec(
            num_scalar_prefetch=1,
            grid=(labels // width,),
            in_specs=[
                pl.BlockSpec((rows, depth), lambda i, p: (0, 0)),
                pl.BlockSpec((width, depth), lambda i, p: (i, 0)),
                pl.BlockSpec((1, width), lambda i, p: (0, i)),
                pl.BlockSpec(ints.shape, lambda i, p: (0, 0)),
            ],
            out_specs=[
                pl.BlockSpec((docs + 8, half), lambda i, p: (0, 0)),
                pl.BlockSpec((docs + 8, half), lambda i, p: (0, 0)),
                pl.BlockSpec((1, width), lambda i, p: (0, i)),
            ],
        ),
        out_shape=[
            jax.ShapeDtypeStruct((docs + 8, half), jnp.float32),
            jax.ShapeDtypeStruct((docs + 8, half), jnp.float32),
            jax.ShapeDtypeStruct((1, labels), jnp.float32),
        ],
        compiler_params=pltpu.CompilerParams(dimension_semantics=("arbitrary",)),
    )(place, emb, label_matrix, log_rates, ints)


def tail_kernel(upper_ref, mine_ref, other_ref, pre_ref, pooled_t_ref, weight_ref, loss_ref):
    upper = upper_ref[0] == 1
    docs = pooled_t_ref.shape[1]
    half = mine_ref.shape[1]
    mine = mine_ref[...]
    other = other_ref[...]
    low = jnp.where(upper, other, mine)
    high = jnp.where(upper, mine, other)
    total = low[docs : docs + 1, 0:1]
    loss_ref[...] = low[docs : docs + 1, 1:2] / total
    pre = pre_ref[docs:, :]
    inv = lax.rsqrt(jnp.sum(pre * pre, axis=1, keepdims=True) + 1e-06)
    unit = pre * inv
    grad_low = low[:docs] * 16.0 / total
    grad_high = high[:docs] * 16.0 / total
    along = jnp.sum(unit[:, :half] * grad_low, axis=1, keepdims=True) + jnp.sum(
        unit[:, half:] * grad_high, axis=1, keepdims=True
    )
    pooled_t = pooled_t_ref[...]
    for index, grad in enumerate((grad_low, grad_high)):
        pre = (grad - unit[:, index * half : (index + 1) * half] * along) * inv
        first = pre.astype(jnp.bfloat16)
        rest = pre - first.astype(jnp.float32)
        second = rest.astype(jnp.bfloat16)
        third = (rest - second.astype(jnp.float32)).astype(jnp.bfloat16)
        acc = jnp.dot(pooled_t, first, preferred_element_type=jnp.float32)
        acc = acc + jnp.dot(pooled_t, second, preferred_element_type=jnp.float32)
        acc = acc + jnp.dot(pooled_t, third, preferred_element_type=jnp.float32)
        weight_ref[:, index * half : (index + 1) * half] = acc


def tail_pass(upper, mine, other, pre, pooled_t):
    depth = pooled_t.shape[0]
    vmem = pltpu.MemorySpace.VMEM
    return pl.pallas_call(
        tail_kernel,
        in_specs=[pl.BlockSpec(memory_space=pltpu.MemorySpace.SMEM)] + [pl.BlockSpec(memory_space=vmem)] * 4,
        out_specs=[pl.BlockSpec(memory_space=vmem), pl.BlockSpec(memory_space=vmem)],
        out_shape=[
            jax.ShapeDtypeStruct((depth, depth), jnp.float32),
            jax.ShapeDtypeStruct((1, 1), jnp.float32),
        ],
    )(upper, mine, other, pre, pooled_t)


def split_sum(keep, send, n, pair_step):
    swap = [(i, i ^ pair_step) for i in range(n)]
    x = keep + lax.ppermute(send, AXES, swap)
    step = 1
    while step < n:
        if step != pair_step:
            x = x + lax.ppermute(x, AXES, [(i, i ^ step) for i in range(n)])
        step *= 2
    return x, lax.ppermute(x, AXES, swap)


def make_shards(n, n_label):
    def shards(
        token_ids, labeled, positive_ids, vocab_table, enc_weight, label_matrix, label_log_rates
    ):
        own_docs, views, title = token_ids.shape
        n_pos = positive_ids.shape[1]
        vocab_rows, width = vocab_table.shape
        label_rows = label_matrix.shape[0]
        me = lax.axis_index(AXES)
        docs = own_docs * n

        packed = jnp.concatenate(
            [token_ids.reshape(own_docs, views * title), positive_ids, labeled[:, None]], axis=1
        )
        spread = jnp.broadcast_to(packed[None], (n,) + packed.shape)
        every = lax.all_to_all(spread, AXES, 0, 0, tiled=False).reshape(docs, packed.shape[1])
        all_tokens = every[:, : views * title].reshape(docs, views, title)

        rows = jnp.transpose(all_tokens, (1, 0, 2)).reshape(views * docs, title) - me * vocab_rows
        codes = jnp.arange(vocab_rows, dtype=jnp.int32)
        tally = jnp.zeros((views * docs, vocab_rows), jnp.float32)
        for position in range(title):
            tally = tally + (rows[:, position : position + 1] == codes[None, :]).astype(jnp.float32)
        partial = jnp.dot(tally.astype(jnp.bfloat16), vocab_table, preferred_element_type=jnp.float32)
        pooled = (tree_sum(partial, n, n_label) * (1.0 / title)).astype(jnp.bfloat16)

        pre = jnp.dot(pooled, enc_weight, preferred_element_type=jnp.float32)
        inv_norm = lax.rsqrt(jnp.sum(pre * pre, axis=-1, keepdims=True) + 1e-06)
        unit = pre * inv_norm
        emb = unit.astype(jnp.bfloat16)

        upper = (me // n_label) % 2
        place = jnp.stack([upper, me * label_rows]).astype(jnp.int32)
        keep, send, new_rates = label_pass(
            place, emb, label_matrix, label_log_rates[None, :], every, views * title
        )
        new_log_rates = new_rates[0]

        mine, other = split_sum(keep, send, n, n_label)
        grad_weight, loss = tail_pass(
            upper.astype(jnp.int32)[None], mine, other, pre, pooled[docs:].T
        )
        loss = loss.reshape(())
        return (loss, grad_weight, new_log_rates)

    return shards


def solution(mesh):
    n = mesh.shape["dp"] * mesh.shape["label"]
    assert n & (n - 1) == 0, "n not pow2"
    return jax.shard_map(
        make_shards(n, mesh.shape["label"]),
        mesh=mesh,
        in_specs=(
            P(AXES, None, None),
            P(AXES),
            P(AXES, None),
            P(AXES, None),
            P(),
            P(AXES, None),
            P(AXES),
        ),
        out_specs=(P(), P(), P(AXES)),
        check_vma=False,
    )
```

```python
import functools

import jax
import jax.numpy as jnp
from jax import lax
from jax.experimental import pallas as pl
from jax.experimental.pallas import tpu as pltpu
from jax.sharding import PartitionSpec as P

AXES = ("dp", "label")


def tree_sum(x, n, n_label):
    me = lax.axis_index(AXES)
    upper = (me // n_label) % 2 == 1
    half = x.shape[1] // 2
    low, high = x[:, :half], x[:, half:]
    swap = [(i, i ^ n_label) for i in range(n)]
    x = jnp.where(upper, high, low) + lax.ppermute(jnp.where(upper, low, high), AXES, swap)
    rows = x.shape[0]
    part = lax.all_to_all(x.reshape(n_label, rows // n_label, half), "label", 0, 0, tiled=False)
    part = jnp.sum(part, axis=0)
    step = 2 * n_label
    while step < n:
        part = part + lax.ppermute(part, AXES, [(i, i ^ step) for i in range(n)])
        step *= 2
    every = jnp.broadcast_to(part[None], (n_label,) + part.shape)
    x = lax.all_to_all(every, "label", 0, 0, tiled=False).reshape(rows, half)
    other = lax.ppermute(x, AXES, swap)
    return jnp.where(upper, jnp.concatenate([other, x], 1), jnp.concatenate([x, other], 1))


def label_kernel(first, place_ref, pre_ref, lab_ref, rate_ref, ints_ref, keep_ref, send_ref, rate_out_ref, emb_ref):
    tile = pl.program_id(0)
    upper = place_ref[0] == 1
    base = place_ref[1]
    docs, half = send_ref.shape[0] - 8, send_ref.shape[1]
    width = lab_ref.shape[0]
    n_pos = ints_ref.shape[1] - 1 - first
    lab = lab_ref[...]

    @pl.when(tile == 0)
    def _():
        pre = pre_ref[...]
        inv_norm = lax.rsqrt(jnp.sum(pre * pre, axis=-1, keepdims=True) + 1e-06)
        emb_ref[...] = (pre * inv_norm).astype(jnp.bfloat16)

    scores = (
        lax.dot_general(emb_ref[...], lab, (((1,), (1,)), ((), ())), preferred_element_type=jnp.float32)
        * 16.0
        - 6.0
    )
    weak = scores[:docs]
    strong = scores[docs:]
    teacher = jax.nn.sigmoid(weak)
    mean_teacher = jnp.sum(teacher, axis=0, keepdims=True) / docs
    codes = base + tile * width + lax.broadcasted_iota(jnp.int32, (1, width), 1)
    ints = ints_ref[...]
    hit = ints[:, first : first + 1] == codes
    for column in range(first + 1, first + n_pos):
        hit = hit | (ints[:, column : column + 1] == codes)
    hit = hit.astype(jnp.float32)
    flag = (ints[:, first + n_pos : first + n_pos + 1] == 1).astype(jnp.float32)
    target = jnp.where(flag > 0.5, hit, teacher * jnp.exp(rate_ref[...]) / mean_teacher)
    softplus = jnp.maximum(strong, 0.0) + jnp.log1p(jnp.exp(-jnp.abs(strong)))
    slope = (jax.nn.sigmoid(strong) - target).astype(jnp.bfloat16)
    count = jnp.sum(ints[:, first + n_pos : first + n_pos + 1].astype(jnp.float32))
    batch_rate = jnp.sum(flag * hit, axis=0, keepdims=True) / count
    rate_out_ref[...] = jnp.log(0.9 * jnp.exp(rate_ref[...]) + 0.1 * batch_rate)
    part = jnp.dot(slope, lab, preferred_element_type=jnp.float32)
    low, high = part[:, :half], part[:, half:]
    lane = lax.broadcasted_iota(jnp.int32, (8, half), 1)
    row = lax.broadcasted_iota(jnp.int32, (8, half), 0)
    total = jnp.sum(target)
    loss = jnp.sum(softplus - target * strong)
    extra = jnp.where(row == 0, jnp.where(lane == 0, total, jnp.where(lane == 1, loss, 0.0)), 0.0)
    keep = jnp.concatenate([jnp.where(upper, high, low), jnp.where(upper, 0.0, extra)], axis=0)
    send = jnp.concatenate([jnp.where(upper, low, high), jnp.where(upper, extra, 0.0)], axis=0)

    @pl.when(tile == 0)
    def _():
        keep_ref[...] = keep
        send_ref[...] = send

    @pl.when(tile > 0)
    def _():
        keep_ref[...] += keep
        send_ref[...] += send


def label_pass(place, pre, label_matrix, log_rates, ints, first):
    rows, depth = pre.shape
    docs = ints.shape[0]
    labels = label_matrix.shape[0]
    width = 1024 if labels % 1024 == 0 else labels
    half = depth // 2
    return pl.pallas_call(
        functools.partial(label_kernel, first),
        grid_spec=pltpu.PrefetchScalarGridSpec(
            num_scalar_prefetch=1,
            grid=(labels // width,),
            in_specs=[
                pl.BlockSpec((rows, depth), lambda i, p: (0, 0)),
                pl.BlockSpec((width, depth), lambda i, p: (i, 0)),
                pl.BlockSpec((1, width), lambda i, p: (0, i)),
                pl.BlockSpec(ints.shape, lambda i, p: (0, 0)),
            ],
            out_specs=[
                pl.BlockSpec((docs + 8, half), lambda i, p: (0, 0)),
                pl.BlockSpec((docs + 8, half), lambda i, p: (0, 0)),
                pl.BlockSpec((1, width), lambda i, p: (0, i)),
            ],
            scratch_shapes=[pltpu.VMEM((rows, depth), jnp.bfloat16)],
        ),
        out_shape=[
            jax.ShapeDtypeStruct((docs + 8, half), jnp.float32),
            jax.ShapeDtypeStruct((docs + 8, half), jnp.float32),
            jax.ShapeDtypeStruct((1, labels), jnp.float32),
        ],
        compiler_params=pltpu.CompilerParams(dimension_semantics=("arbitrary",)),
    )(place, pre, label_matrix, log_rates, ints)


def tail_kernel(upper_ref, mine_ref, other_ref, pre_ref, pooled_t_ref, weight_ref, loss_ref):
    upper = upper_ref[0] == 1
    docs = pooled_t_ref.shape[1]
    half = mine_ref.shape[1]
    mine = mine_ref[...]
    other = other_ref[...]
    low = jnp.where(upper, other, mine)
    high = jnp.where(upper, mine, other)
    total = low[docs : docs + 1, 0:1]
    loss_ref[...] = low[docs : docs + 1, 1:2] / total
    pre = pre_ref[docs:, :]
    inv = lax.rsqrt(jnp.sum(pre * pre, axis=1, keepdims=True) + 1e-06)
    unit = pre * inv
    grad_low = low[:docs] * 16.0 / total
    grad_high = high[:docs] * 16.0 / total
    along = jnp.sum(unit[:, :half] * grad_low, axis=1, keepdims=True) + jnp.sum(
        unit[:, half:] * grad_high, axis=1, keepdims=True
    )
    pooled_t = pooled_t_ref[...]
    for index, grad in enumerate((grad_low, grad_high)):
        pre = (grad - unit[:, index * half : (index + 1) * half] * along) * inv
        first = pre.astype(jnp.bfloat16)
        rest = pre - first.astype(jnp.float32)
        second = rest.astype(jnp.bfloat16)
        third = (rest - second.astype(jnp.float32)).astype(jnp.bfloat16)
        acc = jnp.dot(pooled_t, first, preferred_element_type=jnp.float32)
        acc = acc + jnp.dot(pooled_t, second, preferred_element_type=jnp.float32)
        acc = acc + jnp.dot(pooled_t, third, preferred_element_type=jnp.float32)
        weight_ref[:, index * half : (index + 1) * half] = acc


def tail_pass(upper, mine, other, pre, pooled_t):
    depth = pooled_t.shape[0]
    vmem = pltpu.MemorySpace.VMEM
    return pl.pallas_call(
        tail_kernel,
        in_specs=[pl.BlockSpec(memory_space=pltpu.MemorySpace.SMEM)] + [pl.BlockSpec(memory_space=vmem)] * 4,
        out_specs=[pl.BlockSpec(memory_space=vmem), pl.BlockSpec(memory_space=vmem)],
        out_shape=[
            jax.ShapeDtypeStruct((depth, depth), jnp.float32),
            jax.ShapeDtypeStruct((1, 1), jnp.float32),
        ],
    )(upper, mine, other, pre, pooled_t)


def split_sum(keep, send, n, pair_step):
    swap = [(i, i ^ pair_step) for i in range(n)]
    x = keep + lax.ppermute(send, AXES, swap)
    step = 1
    while step < n:
        if step != pair_step:
            x = x + lax.ppermute(x, AXES, [(i, i ^ step) for i in range(n)])
        step *= 2
    return x, lax.ppermute(x, AXES, swap)


def make_shards(n, n_label):
    def shards(
        token_ids, labeled, positive_ids, vocab_table, enc_weight, label_matrix, label_log_rates
    ):
        own_docs, views, title = token_ids.shape
        n_pos = positive_ids.shape[1]
        vocab_rows, width = vocab_table.shape
        label_rows = label_matrix.shape[0]
        me = lax.axis_index(AXES)
        docs = own_docs * n

        packed = jnp.concatenate(
            [token_ids.reshape(own_docs, views * title), positive_ids, labeled[:, None]], axis=1
        )
        spread = jnp.broadcast_to(packed[None], (n,) + packed.shape)
        every = lax.all_to_all(spread, AXES, 0, 0, tiled=False).reshape(docs, packed.shape[1])
        all_tokens = every[:, : views * title].reshape(docs, views, title)

        rows = jnp.transpose(all_tokens, (1, 0, 2)).reshape(views * docs, title) - me * vocab_rows
        codes = jnp.arange(vocab_rows, dtype=jnp.int32)
        tally = jnp.zeros((views * docs, vocab_rows), jnp.float32)
        for position in range(title):
            tally = tally + (rows[:, position : position + 1] == codes[None, :]).astype(jnp.float32)
        partial = jnp.dot(tally.astype(jnp.bfloat16), vocab_table, preferred_element_type=jnp.float32)
        pooled = (tree_sum(partial, n, n_label) * (1.0 / title)).astype(jnp.bfloat16)

        pre = jnp.dot(pooled, enc_weight, preferred_element_type=jnp.float32)

        upper = (me // n_label) % 2
        place = jnp.stack([upper, me * label_rows]).astype(jnp.int32)
        keep, send, new_rates = label_pass(
            place, pre, label_matrix, label_log_rates[None, :], every, views * title
        )
        new_log_rates = new_rates[0]

        mine, other = split_sum(keep, send, n, n_label)
        grad_weight, loss = tail_pass(
            upper.astype(jnp.int32)[None], mine, other, pre, pooled[docs:].T
        )
        loss = loss.reshape(())
        return (loss, grad_weight, new_log_rates)

    return shards


def solution(mesh):
    n = mesh.shape["dp"] * mesh.shape["label"]
    assert n & (n - 1) == 0, "n not pow2"
    return jax.shard_map(
        make_shards(n, mesh.shape["label"]),
        mesh=mesh,
        in_specs=(
            P(AXES, None, None),
            P(AXES),
            P(AXES, None),
            P(AXES, None),
            P(),
            P(AXES, None),
            P(AXES),
        ),
        out_specs=(P(), P(), P(AXES)),
        check_vma=False,
    )
```

```python
import functools

import jax
import jax.numpy as jnp
from jax import lax
from jax.experimental import pallas as pl
from jax.experimental.pallas import tpu as pltpu
from jax.sharding import PartitionSpec as P

AXES = ("dp", "label")


def tree_sum(x, n, n_label):
    me = lax.axis_index(AXES)
    upper = (me // n_label) % 2 == 1
    half = x.shape[1] // 2
    low, high = x[:, :half], x[:, half:]
    swap = [(i, i ^ n_label) for i in range(n)]
    x = jnp.where(upper, high, low) + lax.ppermute(jnp.where(upper, low, high), AXES, swap)
    rows = x.shape[0]
    part = lax.all_to_all(x.reshape(n_label, rows // n_label, half), "label", 0, 0, tiled=False)
    part = jnp.sum(part, axis=0)
    step = 2 * n_label
    while step < n:
        part = part + lax.ppermute(part, AXES, [(i, i ^ step) for i in range(n)])
        step *= 2
    every = jnp.broadcast_to(part[None], (n_label,) + part.shape)
    x = lax.all_to_all(every, "label", 0, 0, tiled=False).reshape(rows, half)
    other = lax.ppermute(x, AXES, swap)
    return jnp.where(upper, jnp.concatenate([other, x], 1), jnp.concatenate([x, other], 1))


def label_kernel(first, place_ref, emb_ref, lab_ref, rate_ref, ints_ref, keep_ref, send_ref, rate_out_ref):
    tile = pl.program_id(0)
    upper = place_ref[0] == 1
    base = place_ref[1]
    docs, half = send_ref.shape[0] - 8, send_ref.shape[1]
    width = lab_ref.shape[0]
    n_pos = ints_ref.shape[1] - 1 - first
    lab = lab_ref[...]
    scores = (
        lax.dot_general(emb_ref[...], lab, (((1,), (1,)), ((), ())), preferred_element_type=jnp.float32)
        * 16.0
        - 6.0
    )
    weak = scores[:docs]
    strong = scores[docs:]
    teacher = jax.nn.sigmoid(weak)
    mean_teacher = jnp.sum(teacher, axis=0, keepdims=True) / docs
    codes = base + tile * width + lax.broadcasted_iota(jnp.int32, (1, width), 1)
    ints = ints_ref[...]
    hit = ints[:, first : first + 1] == codes
    for column in range(first + 1, first + n_pos):
        hit = hit | (ints[:, column : column + 1] == codes)
    hit = hit.astype(jnp.float32)
    flag = (ints[:, first + n_pos : first + n_pos + 1] == 1).astype(jnp.float32)
    target = jnp.where(flag > 0.5, hit, teacher * jnp.exp(rate_ref[...]) / mean_teacher)
    softplus = jnp.maximum(strong, 0.0) + jnp.log1p(jnp.exp(-jnp.abs(strong)))
    slope = (jax.nn.sigmoid(strong) - target).astype(jnp.bfloat16)
    count = jnp.sum(ints[:, first + n_pos : first + n_pos + 1].astype(jnp.float32))
    batch_rate = jnp.sum(flag * hit, axis=0, keepdims=True) / count
    rate_out_ref[...] = jnp.log(0.9 * jnp.exp(rate_ref[...]) + 0.1 * batch_rate)
    part = jnp.dot(slope, lab, preferred_element_type=jnp.float32)
    low, high = part[:, :half], part[:, half:]
    lane = lax.broadcasted_iota(jnp.int32, (8, half), 1)
    row = lax.broadcasted_iota(jnp.int32, (8, half), 0)
    total = jnp.sum(target)
    loss = jnp.sum(softplus - target * strong)
    extra = jnp.where(row == 0, jnp.where(lane == 0, total, jnp.where(lane == 1, loss, 0.0)), 0.0)
    keep = jnp.concatenate([jnp.where(upper, high, low), jnp.where(upper, 0.0, extra)], axis=0)
    send = jnp.concatenate([jnp.where(upper, low, high), jnp.where(upper, extra, 0.0)], axis=0)

    @pl.when(tile == 0)
    def _():
        keep_ref[...] = keep
        send_ref[...] = send

    @pl.when(tile > 0)
    def _():
        keep_ref[...] += keep
        send_ref[...] += send


def label_pass(place, emb, label_matrix, log_rates, ints, first):
    rows, depth = emb.shape
    docs = ints.shape[0]
    labels = label_matrix.shape[0]
    width = 1024 if labels % 1024 == 0 else labels
    half = depth // 2
    return pl.pallas_call(
        functools.partial(label_kernel, first),
        grid_spec=pltpu.PrefetchScalarGridSpec(
            num_scalar_prefetch=1,
            grid=(labels // width,),
            in_specs=[
                pl.BlockSpec((rows, depth), lambda i, p: (0, 0)),
                pl.BlockSpec((width, depth), lambda i, p: (i, 0)),
                pl.BlockSpec((1, width), lambda i, p: (0, i)),
                pl.BlockSpec(ints.shape, lambda i, p: (0, 0)),
            ],
            out_specs=[
                pl.BlockSpec((docs + 8, half), lambda i, p: (0, 0)),
                pl.BlockSpec((docs + 8, half), lambda i, p: (0, 0)),
                pl.BlockSpec((1, width), lambda i, p: (0, i)),
            ],
        ),
        out_shape=[
            jax.ShapeDtypeStruct((docs + 8, half), jnp.float32),
            jax.ShapeDtypeStruct((docs + 8, half), jnp.float32),
            jax.ShapeDtypeStruct((1, labels), jnp.float32),
        ],
        compiler_params=pltpu.CompilerParams(dimension_semantics=("arbitrary",)),
    )(place, emb, label_matrix, log_rates, ints)


def tail_kernel(upper_ref, mine_ref, other_ref, pre_ref, pooled_t_ref, weight_ref, loss_ref):
    upper = upper_ref[0] == 1
    docs = pooled_t_ref.shape[1]
    half = mine_ref.shape[1]
    mine = mine_ref[...]
    other = other_ref[...]
    low = jnp.where(upper, other, mine)
    high = jnp.where(upper, mine, other)
    total = low[docs : docs + 1, 0:1]
    loss_ref[...] = low[docs : docs + 1, 1:2] / total
    pre = pre_ref[docs:, :]
    inv = lax.rsqrt(jnp.sum(pre * pre, axis=1, keepdims=True) + 1e-06)
    unit = pre * inv
    grad_low = low[:docs] * 16.0 / total
    grad_high = high[:docs] * 16.0 / total
    along = jnp.sum(unit[:, :half] * grad_low, axis=1, keepdims=True) + jnp.sum(
        unit[:, half:] * grad_high, axis=1, keepdims=True
    )
    pooled_t = pooled_t_ref[...]
    for index, grad in enumerate((grad_low, grad_high)):
        pre = (grad - unit[:, index * half : (index + 1) * half] * along) * inv
        first = pre.astype(jnp.bfloat16)
        rest = pre - first.astype(jnp.float32)
        second = rest.astype(jnp.bfloat16)
        third = (rest - second.astype(jnp.float32)).astype(jnp.bfloat16)
        acc = jnp.dot(pooled_t, first, preferred_element_type=jnp.float32)
        acc = acc + jnp.dot(pooled_t, second, preferred_element_type=jnp.float32)
        acc = acc + jnp.dot(pooled_t, third, preferred_element_type=jnp.float32)
        weight_ref[:, index * half : (index + 1) * half] = acc


def tail_pass(upper, mine, other, pre, pooled_t):
    depth = pooled_t.shape[0]
    vmem = pltpu.MemorySpace.VMEM
    return pl.pallas_call(
        tail_kernel,
        in_specs=[pl.BlockSpec(memory_space=pltpu.MemorySpace.SMEM)] + [pl.BlockSpec(memory_space=vmem)] * 4,
        out_specs=[pl.BlockSpec(memory_space=vmem), pl.BlockSpec(memory_space=vmem)],
        out_shape=[
            jax.ShapeDtypeStruct((depth, depth), jnp.float32),
            jax.ShapeDtypeStruct((1, 1), jnp.float32),
        ],
    )(upper, mine, other, pre, pooled_t)


def split_sum(keep, send, n, pair_step, carry):
    swap = [(i, i ^ pair_step) for i in range(n)]
    x = keep + lax.ppermute(send, AXES, swap)
    step = 1
    while step < n:
        if step != pair_step:
            x = x + lax.ppermute(x, AXES, [(i, i ^ step) for i in range(n)])
            if step == 1:
                x, carry = lax.optimization_barrier((x, carry))
        step *= 2
    return x, lax.ppermute(x, AXES, swap), carry


def make_shards(n, n_label):
    def shards(
        token_ids, labeled, positive_ids, vocab_table, enc_weight, label_matrix, label_log_rates
    ):
        own_docs, views, title = token_ids.shape
        n_pos = positive_ids.shape[1]
        vocab_rows, width = vocab_table.shape
        label_rows = label_matrix.shape[0]
        me = lax.axis_index(AXES)
        docs = own_docs * n

        packed = jnp.concatenate(
            [token_ids.reshape(own_docs, views * title), positive_ids, labeled[:, None]], axis=1
        )
        spread = jnp.broadcast_to(packed[None], (n,) + packed.shape)
        every = lax.all_to_all(spread, AXES, 0, 0, tiled=False).reshape(docs, packed.shape[1])
        all_tokens = every[:, : views * title].reshape(docs, views, title)

        rows = jnp.transpose(all_tokens, (1, 0, 2)).reshape(views * docs, title) - me * vocab_rows
        codes = jnp.arange(vocab_rows, dtype=jnp.int32)
        tally = jnp.zeros((views * docs, vocab_rows), jnp.float32)
        for position in range(title):
            tally = tally + (rows[:, position : position + 1] == codes[None, :]).astype(jnp.float32)
        partial = jnp.dot(tally.astype(jnp.bfloat16), vocab_table, preferred_element_type=jnp.float32)
        pooled = (tree_sum(partial, n, n_label) * (1.0 / title)).astype(jnp.bfloat16)

        pre = jnp.dot(pooled, enc_weight, preferred_element_type=jnp.float32)
        inv_norm = lax.rsqrt(jnp.sum(pre * pre, axis=-1, keepdims=True) + 1e-06)
        unit = pre * inv_norm
        emb = unit.astype(jnp.bfloat16)

        upper = (me // n_label) % 2
        place = jnp.stack([upper, me * label_rows]).astype(jnp.int32)
        keep, send, new_rates = label_pass(
            place, emb, label_matrix, label_log_rates[None, :], every, views * title
        )
        new_log_rates = new_rates[0]

        mine, other, pooled_t = split_sum(keep, send, n, n_label, pooled[docs:].T)
        grad_weight, loss = tail_pass(upper.astype(jnp.int32)[None], mine, other, pre, pooled_t)
        loss = loss.reshape(())
        return (loss, grad_weight, new_log_rates)

    return shards


def solution(mesh):
    n = mesh.shape["dp"] * mesh.shape["label"]
    assert n & (n - 1) == 0, "n not pow2"
    return jax.shard_map(
        make_shards(n, mesh.shape["label"]),
        mesh=mesh,
        in_specs=(
            P(AXES, None, None),
            P(AXES),
            P(AXES, None),
            P(AXES, None),
            P(),
            P(AXES, None),
            P(AXES),
        ),
        out_specs=(P(), P(), P(AXES)),
        check_vma=False,
    )
```

```python
import functools

import jax
import jax.numpy as jnp
from jax import lax
from jax.experimental import pallas as pl
from jax.experimental.pallas import tpu as pltpu
from jax.sharding import PartitionSpec as P

AXES = ("dp", "label")


def tree_sum(x, n, n_label):
    me = lax.axis_index(AXES)
    upper = (me // n_label) % 2 == 1
    half = x.shape[1] // 2
    low, high = x[:, :half], x[:, half:]
    swap = [(i, i ^ n_label) for i in range(n)]
    x = jnp.where(upper, high, low) + lax.ppermute(jnp.where(upper, low, high), AXES, swap)
    rows = x.shape[0]
    part = lax.all_to_all(x.reshape(n_label, rows // n_label, half), "label", 0, 0, tiled=False)
    part = jnp.sum(part, axis=0)
    step = 2 * n_label
    while step < n:
        part = part + lax.ppermute(part, AXES, [(i, i ^ step) for i in range(n)])
        step *= 2
    every = jnp.broadcast_to(part[None], (n_label,) + part.shape)
    x = lax.all_to_all(every, "label", 0, 0, tiled=False).reshape(rows, half)
    other = lax.ppermute(x, AXES, swap)
    return jnp.where(upper, jnp.concatenate([other, x], 1), jnp.concatenate([x, other], 1))


def label_kernel(first, n_label, emb_ref, lab_ref, rate_ref, ints_ref, keep_ref, send_ref, rate_out_ref):
    tile = pl.program_id(0)
    me = lax.axis_index(AXES)
    upper = (me // n_label) % 2 == 1
    base = me * lab_ref.shape[0] * pl.num_programs(0)
    docs, half = send_ref.shape[0] - 8, send_ref.shape[1]
    width = lab_ref.shape[0]
    n_pos = ints_ref.shape[1] - 1 - first
    lab = lab_ref[...]
    scores = (
        lax.dot_general(emb_ref[...], lab, (((1,), (1,)), ((), ())), preferred_element_type=jnp.float32)
        * 16.0
        - 6.0
    )
    weak = scores[:docs]
    strong = scores[docs:]
    teacher = jax.nn.sigmoid(weak)
    mean_teacher = jnp.sum(teacher, axis=0, keepdims=True) / docs
    codes = base + tile * width + lax.broadcasted_iota(jnp.int32, (1, width), 1)
    ints = ints_ref[...]
    hit = ints[:, first : first + 1] == codes
    for column in range(first + 1, first + n_pos):
        hit = hit | (ints[:, column : column + 1] == codes)
    hit = hit.astype(jnp.float32)
    flag = (ints[:, first + n_pos : first + n_pos + 1] == 1).astype(jnp.float32)
    target = jnp.where(flag > 0.5, hit, teacher * jnp.exp(rate_ref[...]) / mean_teacher)
    softplus = jnp.maximum(strong, 0.0) + jnp.log1p(jnp.exp(-jnp.abs(strong)))
    slope = (jax.nn.sigmoid(strong) - target).astype(jnp.bfloat16)
    count = jnp.sum(ints[:, first + n_pos : first + n_pos + 1].astype(jnp.float32))
    batch_rate = jnp.sum(flag * hit, axis=0, keepdims=True) / count
    rate_out_ref[...] = jnp.log(0.9 * jnp.exp(rate_ref[...]) + 0.1 * batch_rate)
    part = jnp.dot(slope, lab, preferred_element_type=jnp.float32)
    low, high = part[:, :half], part[:, half:]
    lane = lax.broadcasted_iota(jnp.int32, (8, half), 1)
    row = lax.broadcasted_iota(jnp.int32, (8, half), 0)
    total = jnp.sum(target)
    loss = jnp.sum(softplus - target * strong)
    extra = jnp.where(row == 0, jnp.where(lane == 0, total, jnp.where(lane == 1, loss, 0.0)), 0.0)
    keep = jnp.concatenate([jnp.where(upper, high, low), jnp.where(upper, 0.0, extra)], axis=0)
    send = jnp.concatenate([jnp.where(upper, low, high), jnp.where(upper, extra, 0.0)], axis=0)

    @pl.when(tile == 0)
    def _():
        keep_ref[...] = keep
        send_ref[...] = send

    @pl.when(tile > 0)
    def _():
        keep_ref[...] += keep
        send_ref[...] += send


def label_pass(emb, label_matrix, log_rates, ints, first, n_label):
    rows, depth = emb.shape
    docs = ints.shape[0]
    labels = label_matrix.shape[0]
    width = 1024 if labels % 1024 == 0 else labels
    half = depth // 2
    return pl.pallas_call(
        functools.partial(label_kernel, first, n_label),
        grid_spec=pl.GridSpec(
            grid=(labels // width,),
            in_specs=[
                pl.BlockSpec((rows, depth), lambda i: (0, 0)),
                pl.BlockSpec((width, depth), lambda i: (i, 0)),
                pl.BlockSpec((1, width), lambda i: (0, i)),
                pl.BlockSpec(ints.shape, lambda i: (0, 0)),
            ],
            out_specs=[
                pl.BlockSpec((docs + 8, half), lambda i: (0, 0)),
                pl.BlockSpec((docs + 8, half), lambda i: (0, 0)),
                pl.BlockSpec((1, width), lambda i: (0, i)),
            ],
        ),
        out_shape=[
            jax.ShapeDtypeStruct((docs + 8, half), jnp.float32),
            jax.ShapeDtypeStruct((docs + 8, half), jnp.float32),
            jax.ShapeDtypeStruct((1, labels), jnp.float32),
        ],
        compiler_params=pltpu.CompilerParams(dimension_semantics=("arbitrary",)),
    )(emb, label_matrix, log_rates, ints)


def tail_kernel(upper_ref, mine_ref, other_ref, pre_ref, pooled_t_ref, weight_ref, loss_ref):
    upper = upper_ref[0] == 1
    docs = pooled_t_ref.shape[1]
    half = mine_ref.shape[1]
    mine = mine_ref[...]
    other = other_ref[...]
    low = jnp.where(upper, other, mine)
    high = jnp.where(upper, mine, other)
    total = low[docs : docs + 1, 0:1]
    loss_ref[...] = low[docs : docs + 1, 1:2] / total
    pre = pre_ref[docs:, :]
    inv = lax.rsqrt(jnp.sum(pre * pre, axis=1, keepdims=True) + 1e-06)
    unit = pre * inv
    grad_low = low[:docs] * 16.0 / total
    grad_high = high[:docs] * 16.0 / total
    along = jnp.sum(unit[:, :half] * grad_low, axis=1, keepdims=True) + jnp.sum(
        unit[:, half:] * grad_high, axis=1, keepdims=True
    )
    pooled_t = pooled_t_ref[...]
    for index, grad in enumerate((grad_low, grad_high)):
        pre = (grad - unit[:, index * half : (index + 1) * half] * along) * inv
        first = pre.astype(jnp.bfloat16)
        rest = pre - first.astype(jnp.float32)
        second = rest.astype(jnp.bfloat16)
        third = (rest - second.astype(jnp.float32)).astype(jnp.bfloat16)
        acc = jnp.dot(pooled_t, first, preferred_element_type=jnp.float32)
        acc = acc + jnp.dot(pooled_t, second, preferred_element_type=jnp.float32)
        acc = acc + jnp.dot(pooled_t, third, preferred_element_type=jnp.float32)
        weight_ref[:, index * half : (index + 1) * half] = acc


def tail_pass(upper, mine, other, pre, pooled_t):
    depth = pooled_t.shape[0]
    vmem = pltpu.MemorySpace.VMEM
    return pl.pallas_call(
        tail_kernel,
        in_specs=[pl.BlockSpec(memory_space=pltpu.MemorySpace.SMEM)] + [pl.BlockSpec(memory_space=vmem)] * 4,
        out_specs=[pl.BlockSpec(memory_space=vmem), pl.BlockSpec(memory_space=vmem)],
        out_shape=[
            jax.ShapeDtypeStruct((depth, depth), jnp.float32),
            jax.ShapeDtypeStruct((1, 1), jnp.float32),
        ],
    )(upper, mine, other, pre, pooled_t)


def split_sum(keep, send, n, pair_step, carry):
    swap = [(i, i ^ pair_step) for i in range(n)]
    x = keep + lax.ppermute(send, AXES, swap)
    step = 1
    while step < n:
        if step != pair_step:
            x = x + lax.ppermute(x, AXES, [(i, i ^ step) for i in range(n)])
            if step == 1:
                x, carry = lax.optimization_barrier((x, carry))
        step *= 2
    return x, lax.ppermute(x, AXES, swap), carry


def make_shards(n, n_label):
    def shards(
        token_ids, labeled, positive_ids, vocab_table, enc_weight, label_matrix, label_log_rates
    ):
        own_docs, views, title = token_ids.shape
        n_pos = positive_ids.shape[1]
        vocab_rows, width = vocab_table.shape
        label_rows = label_matrix.shape[0]
        me = lax.axis_index(AXES)
        docs = own_docs * n

        packed = jnp.concatenate(
            [token_ids.reshape(own_docs, views * title), positive_ids, labeled[:, None]], axis=1
        )
        spread = jnp.broadcast_to(packed[None], (n,) + packed.shape)
        every = lax.all_to_all(spread, AXES, 0, 0, tiled=False).reshape(docs, packed.shape[1])
        all_tokens = every[:, : views * title].reshape(docs, views, title)

        rows = jnp.transpose(all_tokens, (1, 0, 2)).reshape(views * docs, title) - me * vocab_rows
        codes = jnp.arange(vocab_rows, dtype=jnp.int32)
        tally = jnp.zeros((views * docs, vocab_rows), jnp.float32)
        for position in range(title):
            tally = tally + (rows[:, position : position + 1] == codes[None, :]).astype(jnp.float32)
        partial = jnp.dot(tally.astype(jnp.bfloat16), vocab_table, preferred_element_type=jnp.float32)
        pooled = (tree_sum(partial, n, n_label) * (1.0 / title)).astype(jnp.bfloat16)

        pre = jnp.dot(pooled, enc_weight, preferred_element_type=jnp.float32)
        inv_norm = lax.rsqrt(jnp.sum(pre * pre, axis=-1, keepdims=True) + 1e-06)
        unit = pre * inv_norm
        emb = unit.astype(jnp.bfloat16)

        upper = (me // n_label) % 2
        keep, send, new_rates = label_pass(
            emb, label_matrix, label_log_rates[None, :], every, views * title, n_label
        )
        new_log_rates = new_rates[0]

        mine, other, pooled_t = split_sum(keep, send, n, n_label, pooled[docs:].T)
        grad_weight, loss = tail_pass(upper.astype(jnp.int32)[None], mine, other, pre, pooled_t)
        loss = loss.reshape(())
        return (loss, grad_weight, new_log_rates)

    return shards


def solution(mesh):
    n = mesh.shape["dp"] * mesh.shape["label"]
    assert n & (n - 1) == 0, "n not pow2"
    return jax.shard_map(
        make_shards(n, mesh.shape["label"]),
        mesh=mesh,
        in_specs=(
            P(AXES, None, None),
            P(AXES),
            P(AXES, None),
            P(AXES, None),
            P(),
            P(AXES, None),
            P(AXES),
        ),
        out_specs=(P(), P(), P(AXES)),
        check_vma=False,
    )
```

```python
import functools

import jax
import jax.numpy as jnp
from jax import lax
from jax.experimental import pallas as pl
from jax.experimental.pallas import tpu as pltpu
from jax.sharding import PartitionSpec as P

AXES = ("dp", "label")


def tree_sum(x, n, n_label):
    me = lax.axis_index(AXES)
    upper = (me // n_label) % 2 == 1
    half = x.shape[1] // 2
    low, high = x[:, :half], x[:, half:]
    swap = [(i, i ^ n_label) for i in range(n)]
    x = jnp.where(upper, high, low) + lax.ppermute(jnp.where(upper, low, high), AXES, swap)
    rows = x.shape[0]
    part = lax.all_to_all(x.reshape(n_label, rows // n_label, half), "label", 0, 0, tiled=False)
    part = jnp.sum(part, axis=0)
    step = 2 * n_label
    while step < n:
        part = part + lax.ppermute(part, AXES, [(i, i ^ step) for i in range(n)])
        step *= 2
    every = jnp.broadcast_to(part[None], (n_label,) + part.shape)
    x = lax.all_to_all(every, "label", 0, 0, tiled=False).reshape(rows, half)
    other = lax.ppermute(x, AXES, swap)
    return jnp.where(upper, jnp.concatenate([other, x], 1), jnp.concatenate([x, other], 1))


def label_kernel(first, n_label, emb_ref, lab_ref, rate_ref, ints_ref, keep_ref, send_ref, rate_out_ref):
    tile = pl.program_id(0)
    me = lax.axis_index(AXES)
    upper = (me // n_label) % 2 == 1
    base = me * lab_ref.shape[0] * pl.num_programs(0)
    docs, half = send_ref.shape[0] - 8, send_ref.shape[1]
    width = lab_ref.shape[0]
    n_pos = ints_ref.shape[1] - 1 - first
    lab = lab_ref[...]
    scores = (
        lax.dot_general(emb_ref[...], lab, (((1,), (1,)), ((), ())), preferred_element_type=jnp.float32)
        * 16.0
        - 6.0
    )
    weak = scores[:docs]
    strong = scores[docs:]
    teacher = jax.nn.sigmoid(weak)
    mean_teacher = jnp.sum(teacher, axis=0, keepdims=True) / docs
    codes = base + tile * width + lax.broadcasted_iota(jnp.int32, (1, width), 1)
    ints = ints_ref[...]
    hit = ints[:, first : first + 1] == codes
    for column in range(first + 1, first + n_pos):
        hit = hit | (ints[:, column : column + 1] == codes)
    hit = hit.astype(jnp.float32)
    flag = (ints[:, first + n_pos : first + n_pos + 1] == 1).astype(jnp.float32)
    target = jnp.where(flag > 0.5, hit, teacher * jnp.exp(rate_ref[...]) / mean_teacher)
    softplus = jnp.maximum(strong, 0.0) + jnp.log1p(jnp.exp(-jnp.abs(strong)))
    slope = (jax.nn.sigmoid(strong) - target).astype(jnp.bfloat16)
    count = jnp.sum(ints[:, first + n_pos : first + n_pos + 1].astype(jnp.float32))
    batch_rate = jnp.sum(flag * hit, axis=0, keepdims=True) / count
    rate_out_ref[...] = jnp.log(0.9 * jnp.exp(rate_ref[...]) + 0.1 * batch_rate)
    part = jnp.dot(slope, lab, preferred_element_type=jnp.float32)
    low, high = part[:, :half], part[:, half:]
    lane = lax.broadcasted_iota(jnp.int32, (8, half), 1)
    row = lax.broadcasted_iota(jnp.int32, (8, half), 0)
    total = jnp.sum(target)
    loss = jnp.sum(softplus - target * strong)
    extra = jnp.where(row == 0, jnp.where(lane == 0, total, jnp.where(lane == 1, loss, 0.0)), 0.0)
    keep = jnp.concatenate([jnp.where(upper, high, low), jnp.where(upper, 0.0, extra)], axis=0)
    send = jnp.concatenate([jnp.where(upper, low, high), jnp.where(upper, extra, 0.0)], axis=0)

    @pl.when(tile == 0)
    def _():
        keep_ref[...] = keep
        send_ref[...] = send

    @pl.when(tile > 0)
    def _():
        keep_ref[...] += keep
        send_ref[...] += send


def label_pass(emb, label_matrix, log_rates, ints, first, n_label):
    rows, depth = emb.shape
    docs = ints.shape[0]
    labels = label_matrix.shape[0]
    width = 2560 if labels % 2560 == 0 and rows <= 256 else (1024 if labels % 1024 == 0 else labels)
    half = depth // 2
    return pl.pallas_call(
        functools.partial(label_kernel, first, n_label),
        grid_spec=pl.GridSpec(
            grid=(labels // width,),
            in_specs=[
                pl.BlockSpec((rows, depth), lambda i: (0, 0)),
                pl.BlockSpec((width, depth), lambda i: (i, 0)),
                pl.BlockSpec((1, width), lambda i: (0, i)),
                pl.BlockSpec(ints.shape, lambda i: (0, 0)),
            ],
            out_specs=[
                pl.BlockSpec((docs + 8, half), lambda i: (0, 0)),
                pl.BlockSpec((docs + 8, half), lambda i: (0, 0)),
                pl.BlockSpec((1, width), lambda i: (0, i)),
            ],
        ),
        out_shape=[
            jax.ShapeDtypeStruct((docs + 8, half), jnp.float32),
            jax.ShapeDtypeStruct((docs + 8, half), jnp.float32),
            jax.ShapeDtypeStruct((1, labels), jnp.float32),
        ],
        compiler_params=pltpu.CompilerParams(dimension_semantics=("arbitrary",)),
    )(emb, label_matrix, log_rates, ints)


def tail_kernel(upper_ref, mine_ref, other_ref, pre_ref, pooled_t_ref, weight_ref, loss_ref):
    upper = upper_ref[0] == 1
    docs = pooled_t_ref.shape[1]
    half = mine_ref.shape[1]
    mine = mine_ref[...]
    other = other_ref[...]
    low = jnp.where(upper, other, mine)
    high = jnp.where(upper, mine, other)
    total = low[docs : docs + 1, 0:1]
    loss_ref[...] = low[docs : docs + 1, 1:2] / total
    pre = pre_ref[docs:, :]
    inv = lax.rsqrt(jnp.sum(pre * pre, axis=1, keepdims=True) + 1e-06)
    unit = pre * inv
    grad_low = low[:docs] * 16.0 / total
    grad_high = high[:docs] * 16.0 / total
    along = jnp.sum(unit[:, :half] * grad_low, axis=1, keepdims=True) + jnp.sum(
        unit[:, half:] * grad_high, axis=1, keepdims=True
    )
    pooled_t = pooled_t_ref[...]
    for index, grad in enumerate((grad_low, grad_high)):
        pre = (grad - unit[:, index * half : (index + 1) * half] * along) * inv
        first = pre.astype(jnp.bfloat16)
        rest = pre - first.astype(jnp.float32)
        second = rest.astype(jnp.bfloat16)
        third = (rest - second.astype(jnp.float32)).astype(jnp.bfloat16)
        acc = jnp.dot(pooled_t, first, preferred_element_type=jnp.float32)
        acc = acc + jnp.dot(pooled_t, second, preferred_element_type=jnp.float32)
        acc = acc + jnp.dot(pooled_t, third, preferred_element_type=jnp.float32)
        weight_ref[:, index * half : (index + 1) * half] = acc


def tail_pass(upper, mine, other, pre, pooled_t):
    depth = pooled_t.shape[0]
    vmem = pltpu.MemorySpace.VMEM
    return pl.pallas_call(
        tail_kernel,
        in_specs=[pl.BlockSpec(memory_space=pltpu.MemorySpace.SMEM)] + [pl.BlockSpec(memory_space=vmem)] * 4,
        out_specs=[pl.BlockSpec(memory_space=vmem), pl.BlockSpec(memory_space=vmem)],
        out_shape=[
            jax.ShapeDtypeStruct((depth, depth), jnp.float32),
            jax.ShapeDtypeStruct((1, 1), jnp.float32),
        ],
    )(upper, mine, other, pre, pooled_t)


def split_sum(keep, send, n, pair_step, carry):
    swap = [(i, i ^ pair_step) for i in range(n)]
    x = keep + lax.ppermute(send, AXES, swap)
    step = 1
    while step < n:
        if step != pair_step:
            x = x + lax.ppermute(x, AXES, [(i, i ^ step) for i in range(n)])
            if step == 1:
                x, carry = lax.optimization_barrier((x, carry))
        step *= 2
    return x, lax.ppermute(x, AXES, swap), carry


def make_shards(n, n_label):
    def shards(
        token_ids, labeled, positive_ids, vocab_table, enc_weight, label_matrix, label_log_rates
    ):
        own_docs, views, title = token_ids.shape
        n_pos = positive_ids.shape[1]
        vocab_rows, width = vocab_table.shape
        label_rows = label_matrix.shape[0]
        me = lax.axis_index(AXES)
        docs = own_docs * n

        packed = jnp.concatenate(
            [token_ids.reshape(own_docs, views * title), positive_ids, labeled[:, None]], axis=1
        )
        spread = jnp.broadcast_to(packed[None], (n,) + packed.shape)
        every = lax.all_to_all(spread, AXES, 0, 0, tiled=False).reshape(docs, packed.shape[1])
        all_tokens = every[:, : views * title].reshape(docs, views, title)

        rows = jnp.transpose(all_tokens, (1, 0, 2)).reshape(views * docs, title) - me * vocab_rows
        codes = jnp.arange(vocab_rows, dtype=jnp.int32)
        tally = jnp.zeros((views * docs, vocab_rows), jnp.float32)
        for position in range(title):
            tally = tally + (rows[:, position : position + 1] == codes[None, :]).astype(jnp.float32)
        partial = jnp.dot(tally.astype(jnp.bfloat16), vocab_table, preferred_element_type=jnp.float32)
        pooled = (tree_sum(partial, n, n_label) * (1.0 / title)).astype(jnp.bfloat16)

        pre = jnp.dot(pooled, enc_weight, preferred_element_type=jnp.float32)
        inv_norm = lax.rsqrt(jnp.sum(pre * pre, axis=-1, keepdims=True) + 1e-06)
        unit = pre * inv_norm
        emb = unit.astype(jnp.bfloat16)

        upper = (me // n_label) % 2
        keep, send, new_rates = label_pass(
            emb, label_matrix, label_log_rates[None, :], every, views * title, n_label
        )
        new_log_rates = new_rates[0]

        mine, other, pooled_t = split_sum(keep, send, n, n_label, pooled[docs:].T)
        grad_weight, loss = tail_pass(upper.astype(jnp.int32)[None], mine, other, pre, pooled_t)
        loss = loss.reshape(())
        return (loss, grad_weight, new_log_rates)

    return shards


def solution(mesh):
    n = mesh.shape["dp"] * mesh.shape["label"]
    assert n & (n - 1) == 0, "n not pow2"
    return jax.shard_map(
        make_shards(n, mesh.shape["label"]),
        mesh=mesh,
        in_specs=(
            P(AXES, None, None),
            P(AXES),
            P(AXES, None),
            P(AXES, None),
            P(),
            P(AXES, None),
            P(AXES),
        ),
        out_specs=(P(), P(), P(AXES)),
        check_vma=False,
    )
```
